256 devices in a mesh: dp: 8 (over z), section: 2 (over core), round: 16 (over x, y).
Axes of the slice: x: 4, y: 4, z: 8, core: 2. Of those that a mesh axis runs over, the one named last changes fastest.
Arguments:
- syndromes: int32 [16, 840, 2048], P('dp', None, 'round'), may hold values 0 or 1
- lengths: int32 [16], P('dp'), may hold values from 512 to 2048, as said below
- flips: int32 [16, 2048], P('dp', 'round'), may hold values 0 or 1
- embed: bfloat16 [840, 512], replicated, may hold values from -0.4375 to 0.4375
- w_in: bfloat16 [2, 512, 1024], P('section'), may hold values from -0.25 to 0.25
- w_out: bfloat16 [2, 1024, 512], P('section'), may hold values from -0.1875 to 0.1875
- leak: float32 [2, 2048, 512], P('section', 'round'), may hold values from 0 to 1, as said below
- angle: float32 [2, 512], P('section'), may hold values from -3.140625 to 3.140625
- readout: bfloat16 [512], replicated, may hold values from -0.25 to 0.25
Outputs:
- grad_in: float32 [2, 512, 1024], P('section', None, ('dp', 'round'))
- grad_out: float32 [2, 1024, 512], P('section', ('dp', 'round'))
The draws below stay inside these ranges and needn't reach their ends.
Inputs may be any that keep to these rules, and one draw needn't show every extreme that they name: A shot's measured rounds are its first lengths rounds; some shot has all 2048. `leak`: Positive.
All inputs are finite; a program needn't handle non-finite values. No bound on the sum of `syndromes` or of `flips` on one device may be relied on, other than what follows from the above.
Results may differ from the reference program's by a relative error of at most 0.013.
Values may be sent and summed in bfloat16 or wider, within the bound.
No kernel may reach another device: no remote copies, remote signals or barrier semaphores. Data moves between devices by JAX's collectives and lax.ppermute only.
A program may use at most 64 MiB of HBM per device.

```python
import jax
import jax.numpy as jnp
from jax import lax

W = 512
NSTAB = 840
SHOT_DEV = 2
CYCLE_COUNT = 2048
SHOTS = 16


def draw_lengths(key, part):
    drawn = jax.random.randint(key, (SHOTS,), CYCLE_COUNT // 4, CYCLE_COUNT + 1)
    return drawn.at[0].set(CYCLE_COUNT).astype(jnp.int32)


def draw_leak(key, part):
    stochastic_seeds = jax.random.split(key, 7)
    slow_share = 0.5
    slow_channel = jax.random.bernoulli(stochastic_seeds[0], slow_share, (2, 1, W))
    slow_rate = jnp.exp(jax.random.uniform(stochastic_seeds[1], (2, 1, W), minval=jnp.log(0.1), maxval=jnp.log(0.5))) / CYCLE_COUNT
    fast_rate = jnp.exp(jax.random.uniform(stochastic_seeds[2], (2, 1, W), minval=jnp.log(1.0 / 50.0), maxval=jnp.log(1.0 / 30.0)))
    background_probability = jnp.where(slow_channel, slow_rate, fast_rate)
    perturbation_spread = jax.random.uniform(stochastic_seeds[3], (2, CYCLE_COUNT, W), minval=0.4, maxval=1.6)
    span_scaling_factor = jnp.exp(jax.random.uniform(stochastic_seeds[4], (2, 16, 1), minval=jnp.log(0.5), maxval=jnp.log(2.0)))
    span_scaling_factor = jnp.repeat(span_scaling_factor, CYCLE_COUNT // 16, axis=1)
    fault_spell_cycles = jax.random.randint(stochastic_seeds[5], (2, 1, 2), 0, CYCLE_COUNT)
    fault_spell_lengths = jax.random.uniform(stochastic_seeds[6], (2, 1, 2), minval=0.22, maxval=0.69)
    cycle_axis_length = jnp.arange(CYCLE_COUNT, dtype=jnp.int32)[None, :, None]
    fault_spells = jnp.sum(jnp.where(cycle_axis_length == fault_spell_cycles, fault_spell_lengths, 0.0), axis=-1, keepdims=True)
    return (background_probability * perturbation_spread * span_scaling_factor + fault_spells).astype(jnp.float32)


def set_ends(array, own_key, low, top_value):
    longest = array.shape.index(max(array.shape))
    spots = []
    for shift in (0, 1):
        where = [jax.random.randint(jax.random.fold_in(own_key, axis), (), 0, length) for axis, length in enumerate(array.shape)]
        where[longest] = (where[longest] + shift) % array.shape[longest]
        spots.append(tuple(where))
    return array.at[spots[0]].set(low).at[spots[1]].set(top_value)


def block_scale(own_key, dims, cuts, low, top_value):
    gain, own = 1.0, jax.random.fold_in(own_key, 6)
    for axis_at, shards_of in cuts:
        steps = jnp.exp(jax.random.uniform(jax.random.fold_in(own, axis_at), (shards_of,), jnp.float32, low / len(cuts), top_value / len(cuts)))
        gain = gain * jnp.repeat(steps, dims[axis_at] // shards_of).reshape([-1 if axis == axis_at else 1 for axis in range(len(dims))])
    return gain


def scatter_about(own_key, shape, spread, bound, cuts=(), kind=jnp.bfloat16):
    result = jax.random.normal(own_key, shape, jnp.float32) * spread
    if len(cuts) > 0:
        result = block_scale(own_key, shape, cuts, -0.22, 0.18) * result
    return jnp.clip(result, min=-bound, max=bound).astype(kind)


def setup_inputs(seed: int = 0) -> dict:
    key_list = jax.random.split(jax.random.key(seed), 10)
    return {
        "syndromes": set_ends((jax.random.randint(key_list[0], (SHOTS, NSTAB, CYCLE_COUNT), 0, 4) < 1).astype(jnp.int32), jax.random.fold_in(key_list[0], 1), 0, 1),
        "lengths": draw_lengths(jax.random.fold_in(key_list[9], 71), 0),
        "flips": set_ends((jax.random.randint(key_list[2], (SHOTS, CYCLE_COUNT), 0, 2) < 1).astype(jnp.int32), jax.random.fold_in(key_list[2], 1), 0, 1),
        "embed": scatter_about(key_list[3], (NSTAB, W), (NSTAB // 4) ** -0.5, 0.4375),
        "w_in": scatter_about(key_list[4], (2, W, 2 * W), W ** -0.5, 0.25, ((0, 2),)),
        "w_out": scatter_about(key_list[5], (2, 2 * W, W), (2 * W) ** -0.5, 0.1875, ((0, 2),)),
        "leak": draw_leak(jax.random.fold_in(key_list[9], 71), 0),
        "angle": jnp.clip(jax.random.uniform(key_list[7], (2, W), jnp.float32, -3.140625, 3.140625), -3.140625, 3.140625),
        "readout": scatter_about(key_list[8], (W,), W ** -0.5, 0.25),
    }


def inverse_rms(values):
    return lax.rsqrt(lax.optimization_barrier(jnp.mean(values * values, axis=-1, keepdims=True)) + 1e-06)

def layer_forward(inputs, weight_in, weight_out, forget, rotation, valid_rounds):
    feature_count = inputs.shape[-1]
    shot_count, round_count = (inputs.shape[0], inputs.shape[1])
    widened = inputs.astype(jnp.float32)
    inv_scale = inverse_rms(widened)
    normed = (widened * inv_scale).astype(jnp.bfloat16)
    driven = jnp.dot(normed.reshape(shot_count * round_count, feature_count), weight_in, preferred_element_type=jnp.float32).reshape(shot_count, round_count, 2 * feature_count)
    driven = driven * valid_rounds[:, :, None]
    input_gain = jnp.sqrt(-jnp.expm1(-2.0 * forget))
    drive_real = jnp.transpose(driven[:, :, :feature_count] * input_gain, (1, 0, 2))
    drive_imag = jnp.transpose(driven[:, :, feature_count:] * input_gain, (1, 0, 2))
    decay_factor = jnp.exp(-forget)
    trans_real = decay_factor * jnp.cos(rotation)[None, :]
    trans_imag = decay_factor * jnp.sin(rotation)[None, :]

    def advance(carry_state, current):
        carry_real, carry_imag = carry_state
        now_real, now_imag, push_real, push_imag = current
        next_real = now_real * carry_real - now_imag * carry_imag + push_real
        next_imag = now_imag * carry_real + now_real * carry_imag + push_imag
        return ((next_real, next_imag), (next_real, next_imag))
    zero_state = jnp.zeros((shot_count, feature_count), jnp.float32)
    last_state, states = lax.scan(advance, (zero_state, zero_state), (trans_real, trans_imag, drive_real, drive_imag))
    hidden = jnp.concatenate([jnp.transpose(states[0], (1, 0, 2)), jnp.transpose(states[1], (1, 0, 2))], axis=-1).astype(jnp.bfloat16)
    mixed = jnp.dot(hidden.reshape(shot_count * round_count, 2 * feature_count), weight_out, preferred_element_type=jnp.float32).reshape(shot_count, round_count, feature_count)
    outputs = (widened + mixed).astype(jnp.bfloat16)
    return (outputs, normed, hidden, inv_scale)

def layer_backward(inputs, normed, hidden, inv_scale, upstream, weight_in, weight_out, forget, rotation, valid_rounds):
    feature_count = inputs.shape[-1]
    shot_count, round_count = (inputs.shape[0], inputs.shape[1])
    upstream_low = upstream.astype(jnp.bfloat16)
    flat_upstream = upstream_low.reshape(shot_count * round_count, feature_count)
    flat_hidden = hidden.reshape(shot_count * round_count, 2 * feature_count)
    grad_out = jnp.dot(flat_hidden.T, flat_upstream, preferred_element_type=jnp.float32)
    state_grad = jnp.dot(flat_upstream, weight_out.T, preferred_element_type=jnp.float32).reshape(shot_count, round_count, 2 * feature_count)
    decay_factor = jnp.exp(-forget)
    trans_real = decay_factor * jnp.cos(rotation)[None, :]
    trans_imag = decay_factor * jnp.sin(rotation)[None, :]
    input_gain = jnp.sqrt(-jnp.expm1(-2.0 * forget))

    def retreat(carry_state, current):
        carry_real, carry_imag = carry_state
        now_real, now_imag, error_real, error_imag = current
        adjoint_real = error_real + carry_real
        adjoint_imag = error_imag + carry_imag
        passed_real = now_real * adjoint_real + now_imag * adjoint_imag
        passed_imag = now_real * adjoint_imag - now_imag * adjoint_real
        return ((passed_real, passed_imag), (adjoint_real, adjoint_imag))
    zero_state = jnp.zeros((shot_count, feature_count), jnp.float32)
    sequence = (trans_real, trans_imag, jnp.transpose(state_grad[:, :, :feature_count], (1, 0, 2)), jnp.transpose(state_grad[:, :, feature_count:], (1, 0, 2)))
    first_carry, adjoints = lax.scan(retreat, (zero_state, zero_state), sequence, reverse=True)
    adjoint_real = jnp.transpose(adjoints[0], (1, 0, 2))
    adjoint_imag = jnp.transpose(adjoints[1], (1, 0, 2))
    drive_grad = (jnp.concatenate([adjoint_real * input_gain, adjoint_imag * input_gain], axis=-1) * valid_rounds[:, :, None]).astype(jnp.bfloat16)
    flat_drive = drive_grad.reshape(shot_count * round_count, 2 * feature_count)
    flat_normed = normed.reshape(shot_count * round_count, feature_count)
    grad_in = jnp.dot(flat_normed.T, flat_drive, preferred_element_type=jnp.float32)
    normed_grad = jnp.dot(flat_drive, weight_in.T, preferred_element_type=jnp.float32).reshape(shot_count, round_count, feature_count)
    widened = inputs.astype(jnp.float32)
    input_grad = upstream + inv_scale * (normed_grad - widened * inv_scale * inv_scale * lax.optimization_barrier(jnp.mean(normed_grad * widened, axis=-1, keepdims=True)))
    return (grad_in, grad_out, input_grad)

def reference(syndromes, lengths, flips, embed, w_in, w_out, leak, angle, readout):
    shot_total = syndromes.shape[0]
    group_count = shot_total // SHOT_DEV
    round_positions = jnp.arange(CYCLE_COUNT, dtype=jnp.int32)
    embed_wide = embed.astype(jnp.float32)
    readout_wide = readout.astype(jnp.float32)

    def group_step(totals, group_index):
        first_shot = (group_index * SHOT_DEV).astype(jnp.int32)
        group_bits = lax.dynamic_slice_in_dim(syndromes, first_shot, SHOT_DEV, 0).astype(jnp.float32)
        group_lengths = lax.dynamic_slice_in_dim(lengths, first_shot, SHOT_DEV, 0)
        group_flips = lax.dynamic_slice_in_dim(flips, first_shot, SHOT_DEV, 0).astype(jnp.float32)
        valid_rounds = (round_positions[None, :] < group_lengths[:, None]).astype(jnp.float32)
        first_input = jnp.einsum('bsr,sw->brw', group_bits, embed_wide).astype(jnp.bfloat16)
        first_out, first_normed, first_hidden, first_inv = layer_forward(first_input, w_in[0], w_out[0], leak[0], angle[0], valid_rounds)
        second_out, second_normed, second_hidden, second_inv = layer_forward(first_out, w_in[1], w_out[1], leak[1], angle[1], valid_rounds)
        logits = jnp.dot(second_out.reshape(SHOT_DEV * CYCLE_COUNT, W), readout, preferred_element_type=jnp.float32).reshape(SHOT_DEV, CYCLE_COUNT)
        logit_grad = (jax.nn.sigmoid(logits) - group_flips) * valid_rounds / shot_total
        second_upstream = logit_grad[:, :, None] * readout_wide
        second_gin, second_gout, second_input_grad = layer_backward(first_out, second_normed, second_hidden, second_inv, second_upstream, w_in[1], w_out[1], leak[1], angle[1], valid_rounds)
        first_upstream = second_input_grad.astype(jnp.bfloat16).astype(jnp.float32)
        first_gin, first_gout, first_input_grad = layer_backward(first_input, first_normed, first_hidden, first_inv, first_upstream, w_in[0], w_out[0], leak[0], angle[0], valid_rounds)
        total_in, total_out = totals
        total_in = total_in + jnp.stack([first_gin, second_gin])
        total_out = total_out + jnp.stack([first_gout, second_gout])
        return ((total_in, total_out), None)
    start = (jnp.zeros((2, W, 2 * W), jnp.float32), jnp.zeros((2, 2 * W, W), jnp.float32))
    totals, unused = lax.scan(group_step, start, jnp.arange(group_count, dtype=jnp.int32))
    return (totals[0], totals[1])
```

```python
import jax
import jax.numpy as jnp
from jax import lax
from jax.sharding import PartitionSpec as P

MICRO = 1


def entering(shard, axis, combine, identity, reverse):
    peers, position = (lax.axis_size(axis), lax.axis_index(axis))
    common = jnp.broadcast_shapes(*(part.shape for part in shard))
    stacked = jnp.stack([jnp.broadcast_to(part, common) for part in shard])
    everything = lax.all_gather(stacked, axis)
    state = tuple(
        jnp.broadcast_to(jnp.asarray(zero, part.dtype), common) for part, zero in zip(shard, identity)
    )
    for k in range(peers):
        at = peers - 1 - k if reverse else k
        reached = at > position if reverse else at < position
        new = combine(state, tuple(everything[at, i] for i in range(len(shard))))
        state = tuple(jnp.where(reached, a, b) for a, b in zip(new, state))
    return state


def ring_stage(x, axis, n, stride, dim):
    index = lax.axis_index(axis)
    size = lax.axis_size(axis)
    pos = (index // stride) % n

    def moved(j, step):
        at = (j // stride) % n
        return j - at * stride + ((at + step) % n) * stride

    ahead = [(j, moved(j, 1)) for j in range(size)]
    behind = [(j, moved(j, -1)) for j in range(size)]
    chunk = x.shape[dim] // n

    def take(part, c):
        return lax.dynamic_slice_in_dim(part, c * chunk, chunk, dim)

    first, second = x[0:1], x[1:2]
    acc_first = take(first, (pos - 1) % n)
    acc_second = take(second, (pos + 1) % n)
    for step in range(n - 1):
        acc_first = lax.ppermute(acc_first, axis, ahead) + take(first, (pos - step - 2) % n)
        acc_second = lax.ppermute(acc_second, axis, behind) + take(second, (pos + step + 2) % n)
    return jnp.concatenate([acc_first, acc_second], 0)


def reduce_scatter_rows(x):
    rows_round = lax.axis_size("round")
    side = int(round(rows_round ** 0.5))
    x = ring_stage(x, "dp", lax.axis_size("dp"), 1, 1)
    x = ring_stage(x, "round", rows_round // side, side, 1)
    return ring_stage(x, "round", side, 1, 1)


def passed_along(value, axis, steps):
    count = lax.axis_size(axis)
    leading, last = (max(0, -steps), min(count, count - steps))
    return lax.ppermute(value, axis, [(source, source + steps) for source in range(leading, last)])


def combine_pairs(preceding, following):
    first_real, first_imag, first_state_real, first_state_imag = preceding
    second_real, second_imag, second_state_real, second_state_imag = following
    return (
        first_real * second_real - first_imag * second_imag,
        first_real * second_imag + first_imag * second_real,
        second_real * first_state_real - second_imag * first_state_imag + second_state_real,
        second_imag * first_state_real + second_real * first_state_imag + second_state_imag,
    )


def incoming_state(summary, neutral):
    return entering(summary, "round", combine_pairs, neutral, False)


def incoming_adjoint(summary, neutral):
    return entering(summary, "round", combine_pairs, neutral, True)


def neutral_of(summary):
    return (
        jnp.ones_like(summary[0]),
        jnp.zeros_like(summary[1]),
        jnp.zeros_like(summary[2]),
        jnp.zeros_like(summary[3]),
    )


def inverse_rms(values):
    return lax.rsqrt(jnp.mean(values * values, axis=-1, keepdims=True) + 1e-06)


def forward_block(inputs, weight_in, weight_out, trans_real, trans_imag, input_gain, valid_rounds):
    feature_count = inputs.shape[-1]
    widened = inputs.astype(jnp.float32)
    normed = (widened * inverse_rms(widened)).astype(jnp.bfloat16)
    driven = jnp.einsum("brw,wk->brk", normed, weight_in, preferred_element_type=jnp.float32)
    driven = driven * valid_rounds[:, :, None]
    drive_real = driven[:, :, :feature_count] * input_gain
    drive_imag = driven[:, :, feature_count:] * input_gain
    prod_real, prod_imag, local_real, local_imag = lax.associative_scan(
        combine_pairs, (trans_real[None], trans_imag[None], drive_real, drive_imag), axis=1
    )
    summary = (prod_real[:, -1], prod_imag[:, -1], local_real[:, -1], local_imag[:, -1])
    carried = incoming_state(summary, neutral_of(summary))
    carry_real = carried[2][:, None]
    carry_imag = carried[3][:, None]
    state_real = local_real + prod_real * carry_real - prod_imag * carry_imag
    state_imag = local_imag + prod_real * carry_imag + prod_imag * carry_real
    hidden = jnp.concatenate([state_real, state_imag], axis=-1).astype(jnp.bfloat16)
    mixed = jnp.einsum("brk,kw->brw", hidden, weight_out, preferred_element_type=jnp.float32)
    outputs = (widened + mixed).astype(jnp.bfloat16)
    return (outputs, normed, hidden)


def backward_block(
    inputs,
    normed,
    hidden,
    upstream,
    weight_in,
    weight_out,
    trans_real,
    trans_imag,
    input_gain,
    valid_rounds,
):
    feature_count = inputs.shape[-1]
    upstream_low = upstream.astype(jnp.bfloat16)
    grad_out = jnp.einsum("brk,brw->kw", hidden, upstream_low, preferred_element_type=jnp.float32)
    state_grad = jnp.einsum(
        "brw,kw->brk", upstream_low, weight_out, preferred_element_type=jnp.float32
    )
    error_real = state_grad[:, :, :feature_count]
    error_imag = state_grad[:, :, feature_count:]
    back_real = trans_real[None]
    back_imag = -trans_imag[None]
    pushed_real = back_real * error_real - back_imag * error_imag
    pushed_imag = back_real * error_imag + back_imag * error_real
    suffix_real, suffix_imag, local_real, local_imag = lax.associative_scan(
        combine_pairs, (back_real, back_imag, pushed_real, pushed_imag), axis=1, reverse=True
    )
    summary = (suffix_real[:, 0], suffix_imag[:, 0], local_real[:, 0], local_imag[:, 0])
    carried = incoming_adjoint(summary, neutral_of(summary))
    carry_real = carried[2][:, None]
    carry_imag = carried[3][:, None]
    passed_real = local_real + suffix_real * carry_real - suffix_imag * carry_imag
    passed_imag = local_imag + suffix_real * carry_imag + suffix_imag * carry_real
    next_real = jnp.concatenate([passed_real[:, 1:], carry_real], axis=1)
    next_imag = jnp.concatenate([passed_imag[:, 1:], carry_imag], axis=1)
    adjoint_real = error_real + next_real
    adjoint_imag = error_imag + next_imag
    drive_grad = (
        jnp.concatenate([adjoint_real * input_gain, adjoint_imag * input_gain], axis=-1)
        * valid_rounds[:, :, None]
    ).astype(jnp.bfloat16)
    grad_in = jnp.einsum("brk,brw->kw", drive_grad, normed, preferred_element_type=jnp.float32)
    normed_grad = jnp.einsum(
        "brk,wk->brw", drive_grad, weight_in, preferred_element_type=jnp.float32
    )
    widened = inputs.astype(jnp.float32)
    inv_scale = inverse_rms(widened)
    input_grad = upstream + inv_scale * (
        normed_grad
        - widened * inv_scale * inv_scale * jnp.mean(normed_grad * widened, axis=-1, keepdims=True)
    )
    return (grad_in, grad_out, input_grad)


def body(syndromes, lengths, flips, embed, w_in, w_out, leak, angle, readout):
    shots_here = syndromes.shape[0]
    rounds_here = syndromes.shape[2]
    feature_count = embed.shape[1]
    micro_shots = shots_here // MICRO
    shot_total = shots_here * lax.axis_size("dp")
    section_index = lax.axis_index("section")
    first_section = section_index == 0
    positions = lax.axis_index("round") * rounds_here + jnp.arange(rounds_here, dtype=jnp.int32)
    valid_all = (positions[None, :] < lengths[:, None]).astype(jnp.float32)
    weight_in = w_in[0]
    weight_out = w_out[0]
    forget = leak[0]
    decay_factor = jnp.exp(-forget)
    trans_real = decay_factor * jnp.cos(angle[0])[None, :]
    trans_imag = decay_factor * jnp.sin(angle[0])[None, :]
    input_gain = jnp.sqrt(-jnp.expm1(-2.0 * forget))
    readout_wide = readout.astype(jnp.float32)
    received = jnp.zeros((micro_shots, rounds_here, feature_count), jnp.bfloat16)
    saved_ticks = []
    loss_grads = []
    for tick_index in range(MICRO + 1):
        own_index = min(tick_index, MICRO - 1)
        syndrome_bits = syndromes[own_index * micro_shots : (own_index + 1) * micro_shots].astype(
            jnp.bfloat16
        )
        embedded = jnp.einsum(
            "bsr,sw->brw", syndrome_bits, embed, preferred_element_type=jnp.float32
        ).astype(jnp.bfloat16)
        inputs = jnp.where(first_section, embedded, received)
        micro_index = jnp.clip(tick_index - section_index, 0, MICRO - 1)
        valid_rounds = lax.dynamic_slice_in_dim(
            valid_all, micro_index * micro_shots, micro_shots, 0
        )
        outputs, normed, hidden = forward_block(
            inputs, weight_in, weight_out, trans_real, trans_imag, input_gain, valid_rounds
        )
        saved_ticks.append((inputs, normed, hidden, valid_rounds))
        if tick_index >= 1:
            logits = jnp.einsum("brw,w->br", outputs, readout, preferred_element_type=jnp.float32)
            targets = flips[(tick_index - 1) * micro_shots : tick_index * micro_shots].astype(
                jnp.float32
            )
            scaled = (jax.nn.sigmoid(logits) - targets) * valid_rounds / shot_total
            loss_grads.append(scaled[:, :, None] * readout_wide)
        if tick_index < MICRO:
            received = passed_along(outputs, "section", 1)
    grad_in_sum = jnp.zeros((2 * feature_count, feature_count), jnp.float32)
    grad_out_sum = jnp.zeros((2 * feature_count, feature_count), jnp.float32)
    arriving = jnp.zeros((micro_shots, rounds_here, feature_count), jnp.bfloat16)
    for tick_index in range(MICRO + 1):
        later_saved = saved_ticks[min(tick_index + 1, MICRO)]
        earlier = saved_ticks[max(tick_index - 1, 0)]
        picked = tuple(
            (jnp.where(first_section, lower, higher) for higher, lower in zip(later_saved, earlier))
        )
        own_grad = (
            loss_grads[tick_index]
            if tick_index < MICRO
            else jnp.zeros((micro_shots, rounds_here, feature_count), jnp.float32)
        )
        upstream = jnp.where(first_section, arriving.astype(jnp.float32), own_grad)
        grad_in_part, grad_out_part, input_grad = backward_block(
            picked[0],
            picked[1],
            picked[2],
            upstream,
            weight_in,
            weight_out,
            trans_real,
            trans_imag,
            input_gain,
            picked[3],
        )
        grad_in_sum = grad_in_sum + grad_in_part
        grad_out_sum = grad_out_sum + grad_out_part
        if tick_index < MICRO:
            arriving = passed_along(input_grad.astype(jnp.bfloat16), "section", -1)
    reduced = reduce_scatter_rows(jnp.stack([grad_in_sum, grad_out_sum]))
    return (jnp.swapaxes(reduced[0:1], 1, 2), reduced[1:2])


def solution(mesh):
    return jax.shard_map(
        body,
        mesh=mesh,
        in_specs=(
            P("dp", None, "round"),
            P("dp"),
            P("dp", "round"),
            P(),
            P("section", None, None),
            P("section", None, None),
            P("section", "round", None),
            P("section", None),
            P(),
        ),
        out_specs=(P("section", None, ("dp", "round")), P("section", ("dp", "round"), None)),
        check_vma=False,
    )
```

```python
import functools

import jax
import jax.numpy as jnp
from jax import lax
from jax.experimental import pallas as pl
from jax.experimental.pallas import tpu as pltpu
from jax.sharding import PartitionSpec as P

MICRO = 1


def _recurrence_kernel(a_re_ref, a_im_ref, d_re_ref, d_im_ref, p_re_ref, p_im_ref, h_re_ref, h_im_ref, *, reverse):
    rounds, width = a_re_ref.shape
    shots = d_re_ref.shape[0]

    def step(i, carry):
        p_re, p_im, states = carry
        t = rounds - 1 - i if reverse else i
        row = pl.ds(t, 1)
        a_re = a_re_ref[row, :]
        a_im = a_im_ref[row, :]
        next_p_re = p_re * a_re - p_im * a_im
        next_p_im = p_re * a_im + p_im * a_re
        p_re_ref[row, :] = next_p_re
        p_im_ref[row, :] = next_p_im
        moved = []
        for b in range(shots):
            h_re, h_im = states[b]
            new_re = a_re * h_re - a_im * h_im + d_re_ref[b, row, :]
            new_im = a_im * h_re + a_re * h_im + d_im_ref[b, row, :]
            h_re_ref[b, row, :] = new_re
            h_im_ref[b, row, :] = new_im
            moved.append((new_re, new_im))
        return (next_p_re, next_p_im, tuple(moved))

    zero = jnp.zeros((1, width), jnp.float32)
    start = (jnp.ones((1, width), jnp.float32), zero, tuple((zero, zero) for _ in range(shots)))
    lax.fori_loop(0, rounds, step, start, unroll=8)


def recurrence(a_re, a_im, d_re, d_im, reverse=False):
    rounds, width = a_re.shape
    shots = d_re.shape[0]
    vmem = pl.BlockSpec(memory_space=pltpu.VMEM)
    coeff = jax.ShapeDtypeStruct((rounds, width), jnp.float32)
    state = jax.ShapeDtypeStruct((shots, rounds, width), jnp.float32)
    return pl.pallas_call(
        functools.partial(_recurrence_kernel, reverse=reverse),
        out_shape=(coeff, coeff, state, state),
        in_specs=[vmem] * 4,
        out_specs=(vmem,) * 4,
        cost_estimate=pl.CostEstimate(
            flops=8 * rounds * width * (shots + 1),
            transcendentals=0,
            bytes_accessed=4 * 4 * rounds * width * (shots + 1),
        ),
    )(a_re, a_im, d_re, d_im)


def entering(shard, axis, combine, identity, reverse):
    peers, position = (lax.axis_size(axis), lax.axis_index(axis))
    common = jnp.broadcast_shapes(*(part.shape for part in shard))
    stacked = jnp.stack([jnp.broadcast_to(part, common) for part in shard])
    everything = lax.all_gather(stacked, axis)
    state = tuple(
        jnp.broadcast_to(jnp.asarray(zero, part.dtype), common) for part, zero in zip(shard, identity)
    )
    for k in range(peers):
        at = peers - 1 - k if reverse else k
        reached = at > position if reverse else at < position
        new = combine(state, tuple(everything[at, i] for i in range(len(shard))))
        state = tuple(jnp.where(reached, a, b) for a, b in zip(new, state))
    return state


def ring_stage(x, axis, n, stride, dim):
    index = lax.axis_index(axis)
    size = lax.axis_size(axis)
    pos = (index // stride) % n

    def moved(j, step):
        at = (j // stride) % n
        return j - at * stride + ((at + step) % n) * stride

    ahead = [(j, moved(j, 1)) for j in range(size)]
    behind = [(j, moved(j, -1)) for j in range(size)]
    chunk = x.shape[dim] // n

    def take(part, c):
        return lax.dynamic_slice_in_dim(part, c * chunk, chunk, dim)

    first, second = x[0:1], x[1:2]
    acc_first = take(first, (pos - 1) % n)
    acc_second = take(second, (pos + 1) % n)
    for step in range(n - 1):
        acc_first = lax.ppermute(acc_first, axis, ahead) + take(first, (pos - step - 2) % n)
        acc_second = lax.ppermute(acc_second, axis, behind) + take(second, (pos + step + 2) % n)
    return jnp.concatenate([acc_first, acc_second], 0)


def reduce_scatter_rows(x):
    rows_round = lax.axis_size("round")
    side = int(round(rows_round ** 0.5))
    x = ring_stage(x, "dp", lax.axis_size("dp"), 1, 1)
    x = ring_stage(x, "round", rows_round // side, side, 1)
    return ring_stage(x, "round", side, 1, 1)


def passed_along(value, axis, steps):
    count = lax.axis_size(axis)
    leading, last = (max(0, -steps), min(count, count - steps))
    return lax.ppermute(value, axis, [(source, source + steps) for source in range(leading, last)])


def combine_pairs(preceding, following):
    first_real, first_imag, first_state_real, first_state_imag = preceding
    second_real, second_imag, second_state_real, second_state_imag = following
    return (
        first_real * second_real - first_imag * second_imag,
        first_real * second_imag + first_imag * second_real,
        second_real * first_state_real - second_imag * first_state_imag + second_state_real,
        second_imag * first_state_real + second_real * first_state_imag + second_state_imag,
    )


def incoming_state(summary, neutral):
    return entering(summary, "round", combine_pairs, neutral, False)


def incoming_adjoint(summary, neutral):
    return entering(summary, "round", combine_pairs, neutral, True)


def neutral_of(summary):
    return (
        jnp.ones_like(summary[0]),
        jnp.zeros_like(summary[1]),
        jnp.zeros_like(summary[2]),
        jnp.zeros_like(summary[3]),
    )


def inverse_rms(values):
    return lax.rsqrt(jnp.mean(values * values, axis=-1, keepdims=True) + 1e-06)


def forward_block(inputs, weight_in, weight_out, trans_real, trans_imag, input_gain, valid_rounds):
    feature_count = inputs.shape[-1]
    widened = inputs.astype(jnp.float32)
    normed = (widened * inverse_rms(widened)).astype(jnp.bfloat16)
    driven = jnp.einsum("brw,wk->brk", normed, weight_in, preferred_element_type=jnp.float32)
    driven = driven * valid_rounds[:, :, None]
    drive_real = driven[:, :, :feature_count] * input_gain
    drive_imag = driven[:, :, feature_count:] * input_gain
    prod_real, prod_imag, local_real, local_imag = recurrence(
        trans_real, trans_imag, drive_real, drive_imag
    )
    prod_real, prod_imag = (prod_real[None], prod_imag[None])
    summary = (prod_real[:, -1], prod_imag[:, -1], local_real[:, -1], local_imag[:, -1])
    carried = incoming_state(summary, neutral_of(summary))
    carry_real = carried[2][:, None]
    carry_imag = carried[3][:, None]
    state_real = local_real + prod_real * carry_real - prod_imag * carry_imag
    state_imag = local_imag + prod_real * carry_imag + prod_imag * carry_real
    hidden = jnp.concatenate([state_real, state_imag], axis=-1).astype(jnp.bfloat16)
    mixed = jnp.einsum("brk,kw->brw", hidden, weight_out, preferred_element_type=jnp.float32)
    outputs = (widened + mixed).astype(jnp.bfloat16)
    return (outputs, normed, hidden)


def backward_block(
    inputs,
    normed,
    hidden,
    upstream,
    weight_in,
    weight_out,
    trans_real,
    trans_imag,
    input_gain,
    valid_rounds,
):
    feature_count = inputs.shape[-1]
    upstream_low = upstream.astype(jnp.bfloat16)
    grad_out = jnp.einsum("brk,brw->kw", hidden, upstream_low, preferred_element_type=jnp.float32)
    state_grad = jnp.einsum(
        "brw,kw->brk", upstream_low, weight_out, preferred_element_type=jnp.float32
    )
    error_real = state_grad[:, :, :feature_count]
    error_imag = state_grad[:, :, feature_count:]
    back_real = trans_real[None]
    back_imag = -trans_imag[None]
    pushed_real = back_real * error_real - back_imag * error_imag
    pushed_imag = back_real * error_imag + back_imag * error_real
    suffix_real, suffix_imag, local_real, local_imag = recurrence(
        back_real[0], back_imag[0], pushed_real, pushed_imag, reverse=True
    )
    suffix_real, suffix_imag = (suffix_real[None], suffix_imag[None])
    summary = (suffix_real[:, 0], suffix_imag[:, 0], local_real[:, 0], local_imag[:, 0])
    carried = incoming_adjoint(summary, neutral_of(summary))
    carry_real = carried[2][:, None]
    carry_imag = carried[3][:, None]
    passed_real = local_real + suffix_real * carry_real - suffix_imag * carry_imag
    passed_imag = local_imag + suffix_real * carry_imag + suffix_imag * carry_real
    next_real = jnp.concatenate([passed_real[:, 1:], carry_real], axis=1)
    next_imag = jnp.concatenate([passed_imag[:, 1:], carry_imag], axis=1)
    adjoint_real = error_real + next_real
    adjoint_imag = error_imag + next_imag
    drive_grad = (
        jnp.concatenate([adjoint_real * input_gain, adjoint_imag * input_gain], axis=-1)
        * valid_rounds[:, :, None]
    ).astype(jnp.bfloat16)
    grad_in = jnp.einsum("brk,brw->kw", drive_grad, normed, preferred_element_type=jnp.float32)
    normed_grad = jnp.einsum(
        "brk,wk->brw", drive_grad, weight_in, preferred_element_type=jnp.float32
    )
    widened = inputs.astype(jnp.float32)
    inv_scale = inverse_rms(widened)
    input_grad = upstream + inv_scale * (
        normed_grad
        - widened * inv_scale * inv_scale * jnp.mean(normed_grad * widened, axis=-1, keepdims=True)
    )
    return (grad_in, grad_out, input_grad)


def body(syndromes, lengths, flips, embed, w_in, w_out, leak, angle, readout):
    shots_here = syndromes.shape[0]
    rounds_here = syndromes.shape[2]
    feature_count = embed.shape[1]
    micro_shots = shots_here // MICRO
    shot_total = shots_here * lax.axis_size("dp")
    section_index = lax.axis_index("section")
    first_section = section_index == 0
    positions = lax.axis_index("round") * rounds_here + jnp.arange(rounds_here, dtype=jnp.int32)
    valid_all = (positions[None, :] < lengths[:, None]).astype(jnp.float32)
    weight_in = w_in[0]
    weight_out = w_out[0]
    forget = leak[0]
    decay_factor = jnp.exp(-forget)
    trans_real = decay_factor * jnp.cos(angle[0])[None, :]
    trans_imag = decay_factor * jnp.sin(angle[0])[None, :]
    input_gain = jnp.sqrt(-jnp.expm1(-2.0 * forget))
    readout_wide = readout.astype(jnp.float32)
    received = jnp.zeros((micro_shots, rounds_here, feature_count), jnp.bfloat16)
    saved_ticks = []
    loss_grads = []
    for tick_index in range(MICRO + 1):
        own_index = min(tick_index, MICRO - 1)
        syndrome_bits = syndromes[own_index * micro_shots : (own_index + 1) * micro_shots].astype(
            jnp.bfloat16
        )
        embedded = jnp.einsum(
            "bsr,sw->brw", syndrome_bits, embed, preferred_element_type=jnp.float32
        ).astype(jnp.bfloat16)
        inputs = jnp.where(first_section, embedded, received)
        micro_index = jnp.clip(tick_index - section_index, 0, MICRO - 1)
        valid_rounds = lax.dynamic_slice_in_dim(
            valid_all, micro_index * micro_shots, micro_shots, 0
        )
        outputs, normed, hidden = forward_block(
            inputs, weight_in, weight_out, trans_real, trans_imag, input_gain, valid_rounds
        )
        saved_ticks.append((inputs, normed, hidden, valid_rounds))
        if tick_index >= 1:
            logits = jnp.einsum("brw,w->br", outputs, readout, preferred_element_type=jnp.float32)
            targets = flips[(tick_index - 1) * micro_shots : tick_index * micro_shots].astype(
                jnp.float32
            )
            scaled = (jax.nn.sigmoid(logits) - targets) * valid_rounds / shot_total
            loss_grads.append(scaled[:, :, None] * readout_wide)
        if tick_index < MICRO:
            received = passed_along(outputs, "section", 1)
    grad_in_sum = jnp.zeros((2 * feature_count, feature_count), jnp.float32)
    grad_out_sum = jnp.zeros((2 * feature_count, feature_count), jnp.float32)
    arriving = jnp.zeros((micro_shots, rounds_here, feature_count), jnp.bfloat16)
    for tick_index in range(MICRO + 1):
        later_saved = saved_ticks[min(tick_index + 1, MICRO)]
        earlier = saved_ticks[max(tick_index - 1, 0)]
        picked = tuple(
            (jnp.where(first_section, lower, higher) for higher, lower in zip(later_saved, earlier))
        )
        own_grad = (
            loss_grads[tick_index]
            if tick_index < MICRO
            else jnp.zeros((micro_shots, rounds_here, feature_count), jnp.float32)
        )
        upstream = jnp.where(first_section, arriving.astype(jnp.float32), own_grad)
        grad_in_part, grad_out_part, input_grad = backward_block(
            picked[0],
            picked[1],
            picked[2],
            upstream,
            weight_in,
            weight_out,
            trans_real,
            trans_imag,
            input_gain,
            picked[3],
        )
        grad_in_sum = grad_in_sum + grad_in_part
        grad_out_sum = grad_out_sum + grad_out_part
        if tick_index < MICRO:
            arriving = passed_along(input_grad.astype(jnp.bfloat16), "section", -1)
    reduced = reduce_scatter_rows(jnp.stack([grad_in_sum, grad_out_sum]))
    return (jnp.swapaxes(reduced[0:1], 1, 2), reduced[1:2])


def solution(mesh):
    return jax.shard_map(
        body,
        mesh=mesh,
        in_specs=(
            P("dp", None, "round"),
            P("dp"),
            P("dp", "round"),
            P(),
            P("section", None, None),
            P("section", None, None),
            P("section", "round", None),
            P("section", None),
            P(),
        ),
        out_specs=(P("section", None, ("dp", "round")), P("section", ("dp", "round"), None)),
        check_vma=False,
    )
```

```python
import functools

import jax
import jax.numpy as jnp
from jax import lax
from jax.experimental import pallas as pl
from jax.experimental.pallas import tpu as pltpu
from jax.sharding import PartitionSpec as P

MICRO = 1


def _recurrence_kernel(a_re_ref, a_im_ref, d_re_ref, d_im_ref, p_re_ref, p_im_ref, h_re_ref, h_im_ref, *, reverse):
    rounds, width = a_re_ref.shape
    shots = d_re_ref.shape[0]

    def step(i, carry):
        p_re, p_im, states = carry
        t = rounds - 1 - i if reverse else i
        row = pl.ds(t, 1)
        a_re = a_re_ref[row, :]
        a_im = a_im_ref[row, :]
        next_p_re = p_re * a_re - p_im * a_im
        next_p_im = p_re * a_im + p_im * a_re
        p_re_ref[row, :] = next_p_re
        p_im_ref[row, :] = next_p_im
        moved = []
        for b in range(shots):
            h_re, h_im = states[b]
            new_re = a_re * h_re - a_im * h_im + d_re_ref[b, row, :]
            new_im = a_im * h_re + a_re * h_im + d_im_ref[b, row, :]
            h_re_ref[b, row, :] = new_re
            h_im_ref[b, row, :] = new_im
            moved.append((new_re, new_im))
        return (next_p_re, next_p_im, tuple(moved))

    zero = jnp.zeros((1, width), jnp.float32)
    start = (jnp.ones((1, width), jnp.float32), zero, tuple((zero, zero) for _ in range(shots)))
    lax.fori_loop(0, rounds, step, start, unroll=8)


def recurrence(a_re, a_im, d_re, d_im, reverse=False):
    rounds, width = a_re.shape
    shots = d_re.shape[0]
    vmem = pl.BlockSpec(memory_space=pltpu.VMEM)
    coeff = jax.ShapeDtypeStruct((rounds, width), jnp.float32)
    state = jax.ShapeDtypeStruct((shots, rounds, width), jnp.float32)
    return pl.pallas_call(
        functools.partial(_recurrence_kernel, reverse=reverse),
        out_shape=(coeff, coeff, state, state),
        in_specs=[vmem] * 4,
        out_specs=(vmem,) * 4,
        cost_estimate=pl.CostEstimate(
            flops=8 * rounds * width * (shots + 1),
            transcendentals=0,
            bytes_accessed=4 * 4 * rounds * width * (shots + 1),
        ),
    )(a_re, a_im, d_re, d_im)


def entering(shard, axis, combine, identity, reverse):
    peers, position = (lax.axis_size(axis), lax.axis_index(axis))
    common = jnp.broadcast_shapes(*(part.shape for part in shard))
    own = tuple(jnp.broadcast_to(part, common) for part in shard)
    neutral = tuple(
        jnp.broadcast_to(jnp.asarray(zero, part.dtype), common) for part, zero in zip(shard, identity)
    )

    def fetch(value, distance):
        if reverse:
            pairs = [(j, j - distance) for j in range(distance, peers)]
            present = position + distance < peers
        else:
            pairs = [(j, j + distance) for j in range(peers - distance)]
            present = position >= distance
        got = lax.ppermute(jnp.stack(value), axis, pairs)
        return tuple(jnp.where(present, got[i], neutral[i]) for i in range(len(value)))

    if peers == 1:
        return neutral
    state = fetch(own, 1)
    if peers > 2:
        state = combine(fetch(own, 2), state)
    window = 2
    while window < peers:
        state = combine(fetch(state, window), state)
        window *= 2
    return state


def ring_stage(x, axis, n, stride, dim):
    index = lax.axis_index(axis)
    size = lax.axis_size(axis)
    pos = (index // stride) % n

    def moved(j, step):
        at = (j // stride) % n
        return j - at * stride + ((at + step) % n) * stride

    ahead = [(j, moved(j, 1)) for j in range(size)]
    behind = [(j, moved(j, -1)) for j in range(size)]
    chunk = x.shape[dim] // n

    def take(part, c):
        return lax.dynamic_slice_in_dim(part, c * chunk, chunk, dim)

    first, second = x[0:1], x[1:2]
    acc_first = take(first, (pos - 1) % n)
    acc_second = take(second, (pos + 1) % n)
    for step in range(n - 1):
        acc_first = lax.ppermute(acc_first, axis, ahead) + take(first, (pos - step - 2) % n)
        acc_second = lax.ppermute(acc_second, axis, behind) + take(second, (pos + step + 2) % n)
    return jnp.concatenate([acc_first, acc_second], 0)


def reduce_scatter_rows(x):
    rows_round = lax.axis_size("round")
    side = int(round(rows_round ** 0.5))
    x = ring_stage(x, "dp", lax.axis_size("dp"), 1, 1)
    x = ring_stage(x, "round", rows_round // side, side, 1)
    return ring_stage(x, "round", side, 1, 1)


def passed_along(value, axis, steps):
    count = lax.axis_size(axis)
    leading, last = (max(0, -steps), min(count, count - steps))
    return lax.ppermute(value, axis, [(source, source + steps) for source in range(leading, last)])


def combine_pairs(preceding, following):
    first_real, first_imag, first_state_real, first_state_imag = preceding
    second_real, second_imag, second_state_real, second_state_imag = following
    return (
        first_real * second_real - first_imag * second_imag,
        first_real * second_imag + first_imag * second_real,
        second_real * first_state_real - second_imag * first_state_imag + second_state_real,
        second_imag * first_state_real + second_real * first_state_imag + second_state_imag,
    )


def incoming_state(summary, neutral):
    return entering(summary, "round", combine_pairs, neutral, False)


def incoming_adjoint(summary, neutral):
    return entering(summary, "round", combine_pairs, neutral, True)


def neutral_of(summary):
    return (
        jnp.ones_like(summary[0]),
        jnp.zeros_like(summary[1]),
        jnp.zeros_like(summary[2]),
        jnp.zeros_like(summary[3]),
    )


def inverse_rms(values):
    return lax.rsqrt(jnp.mean(values * values, axis=-1, keepdims=True) + 1e-06)


def forward_block(inputs, weight_in, weight_out, trans_real, trans_imag, input_gain, valid_rounds):
    feature_count = inputs.shape[-1]
    widened = inputs.astype(jnp.float32)
    normed = (widened * inverse_rms(widened)).astype(jnp.bfloat16)
    driven = jnp.einsum("brw,wk->brk", normed, weight_in, preferred_element_type=jnp.float32)
    driven = driven * valid_rounds[:, :, None]
    drive_real = driven[:, :, :feature_count] * input_gain
    drive_imag = driven[:, :, feature_count:] * input_gain
    prod_real, prod_imag, local_real, local_imag = recurrence(
        trans_real, trans_imag, drive_real, drive_imag
    )
    prod_real, prod_imag = (prod_real[None], prod_imag[None])
    summary = (prod_real[:, -1], prod_imag[:, -1], local_real[:, -1], local_imag[:, -1])
    carried = incoming_state(summary, neutral_of(summary))
    carry_real = carried[2][:, None]
    carry_imag = carried[3][:, None]
    state_real = local_real + prod_real * carry_real - prod_imag * carry_imag
    state_imag = local_imag + prod_real * carry_imag + prod_imag * carry_real
    hidden = jnp.concatenate([state_real, state_imag], axis=-1).astype(jnp.bfloat16)
    mixed = jnp.einsum("brk,kw->brw", hidden, weight_out, preferred_element_type=jnp.float32)
    outputs = (widened + mixed).astype(jnp.bfloat16)
    return (outputs, normed, hidden)


def backward_block(
    inputs,
    normed,
    hidden,
    upstream,
    weight_in,
    weight_out,
    trans_real,
    trans_imag,
    input_gain,
    valid_rounds,
):
    feature_count = inputs.shape[-1]
    upstream_low = upstream.astype(jnp.bfloat16)
    grad_out = jnp.einsum("brk,brw->kw", hidden, upstream_low, preferred_element_type=jnp.float32)
    state_grad = jnp.einsum(
        "brw,kw->brk", upstream_low, weight_out, preferred_element_type=jnp.float32
    )
    error_real = state_grad[:, :, :feature_count]
    error_imag = state_grad[:, :, feature_count:]
    back_real = trans_real[None]
    back_imag = -trans_imag[None]
    pushed_real = back_real * error_real - back_imag * error_imag
    pushed_imag = back_real * error_imag + back_imag * error_real
    suffix_real, suffix_imag, local_real, local_imag = recurrence(
        back_real[0], back_imag[0], pushed_real, pushed_imag, reverse=True
    )
    suffix_real, suffix_imag = (suffix_real[None], suffix_imag[None])
    summary = (suffix_real[:, 0], suffix_imag[:, 0], local_real[:, 0], local_imag[:, 0])
    carried = incoming_adjoint(summary, neutral_of(summary))
    carry_real = carried[2][:, None]
    carry_imag = carried[3][:, None]
    passed_real = local_real + suffix_real * carry_real - suffix_imag * carry_imag
    passed_imag = local_imag + suffix_real * carry_imag + suffix_imag * carry_real
    next_real = jnp.concatenate([passed_real[:, 1:], carry_real], axis=1)
    next_imag = jnp.concatenate([passed_imag[:, 1:], carry_imag], axis=1)
    adjoint_real = error_real + next_real
    adjoint_imag = error_imag + next_imag
    drive_grad = (
        jnp.concatenate([adjoint_real * input_gain, adjoint_imag * input_gain], axis=-1)
        * valid_rounds[:, :, None]
    ).astype(jnp.bfloat16)
    grad_in = jnp.einsum("brk,brw->kw", drive_grad, normed, preferred_element_type=jnp.float32)
    normed_grad = jnp.einsum(
        "brk,wk->brw", drive_grad, weight_in, preferred_element_type=jnp.float32
    )
    widened = inputs.astype(jnp.float32)
    inv_scale = inverse_rms(widened)
    input_grad = upstream + inv_scale * (
        normed_grad
        - widened * inv_scale * inv_scale * jnp.mean(normed_grad * widened, axis=-1, keepdims=True)
    )
    return (grad_in, grad_out, input_grad)


def body(syndromes, lengths, flips, embed, w_in, w_out, leak, angle, readout):
    shots_here = syndromes.shape[0]
    rounds_here = syndromes.shape[2]
    feature_count = embed.shape[1]
    micro_shots = shots_here // MICRO
    shot_total = shots_here * lax.axis_size("dp")
    section_index = lax.axis_index("section")
    first_section = section_index == 0
    positions = lax.axis_index("round") * rounds_here + jnp.arange(rounds_here, dtype=jnp.int32)
    valid_all = (positions[None, :] < lengths[:, None]).astype(jnp.float32)
    weight_in = w_in[0]
    weight_out = w_out[0]
    forget = leak[0]
    decay_factor = jnp.exp(-forget)
    trans_real = decay_factor * jnp.cos(angle[0])[None, :]
    trans_imag = decay_factor * jnp.sin(angle[0])[None, :]
    input_gain = jnp.sqrt(-jnp.expm1(-2.0 * forget))
    readout_wide = readout.astype(jnp.float32)
    received = jnp.zeros((micro_shots, rounds_here, feature_count), jnp.bfloat16)
    saved_ticks = []
    loss_grads = []
    for tick_index in range(MICRO + 1):
        own_index = min(tick_index, MICRO - 1)
        syndrome_bits = syndromes[own_index * micro_shots : (own_index + 1) * micro_shots].astype(
            jnp.bfloat16
        )
        embedded = jnp.einsum(
            "bsr,sw->brw", syndrome_bits, embed, preferred_element_type=jnp.float32
        ).astype(jnp.bfloat16)
        inputs = jnp.where(first_section, embedded, received)
        micro_index = jnp.clip(tick_index - section_index, 0, MICRO - 1)
        valid_rounds = lax.dynamic_slice_in_dim(
            valid_all, micro_index * micro_shots, micro_shots, 0
        )
        outputs, normed, hidden = forward_block(
            inputs, weight_in, weight_out, trans_real, trans_imag, input_gain, valid_rounds
        )
        saved_ticks.append((inputs, normed, hidden, valid_rounds))
        if tick_index >= 1:
            logits = jnp.einsum("brw,w->br", outputs, readout, preferred_element_type=jnp.float32)
            targets = flips[(tick_index - 1) * micro_shots : tick_index * micro_shots].astype(
                jnp.float32
            )
            scaled = (jax.nn.sigmoid(logits) - targets) * valid_rounds / shot_total
            loss_grads.append(scaled[:, :, None] * readout_wide)
        if tick_index < MICRO:
            received = passed_along(outputs, "section", 1)
    grad_in_sum = jnp.zeros((2 * feature_count, feature_count), jnp.float32)
    grad_out_sum = jnp.zeros((2 * feature_count, feature_count), jnp.float32)
    arriving = jnp.zeros((micro_shots, rounds_here, feature_count), jnp.bfloat16)
    for tick_index in range(MICRO + 1):
        later_saved = saved_ticks[min(tick_index + 1, MICRO)]
        earlier = saved_ticks[max(tick_index - 1, 0)]
        picked = tuple(
            (jnp.where(first_section, lower, higher) for higher, lower in zip(later_saved, earlier))
        )
        own_grad = (
            loss_grads[tick_index]
            if tick_index < MICRO
            else jnp.zeros((micro_shots, rounds_here, feature_count), jnp.float32)
        )
        upstream = jnp.where(first_section, arriving.astype(jnp.float32), own_grad)
        grad_in_part, grad_out_part, input_grad = backward_block(
            picked[0],
            picked[1],
            picked[2],
            upstream,
            weight_in,
            weight_out,
            trans_real,
            trans_imag,
            input_gain,
            picked[3],
        )
        grad_in_sum = grad_in_sum + grad_in_part
        grad_out_sum = grad_out_sum + grad_out_part
        if tick_index < MICRO:
            arriving = passed_along(input_grad.astype(jnp.bfloat16), "section", -1)
    reduced = reduce_scatter_rows(jnp.stack([grad_in_sum, grad_out_sum]))
    return (jnp.swapaxes(reduced[0:1], 1, 2), reduced[1:2])


def solution(mesh):
    return jax.shard_map(
        body,
        mesh=mesh,
        in_specs=(
            P("dp", None, "round"),
            P("dp"),
            P("dp", "round"),
            P(),
            P("section", None, None),
            P("section", None, None),
            P("section", "round", None),
            P("section", None),
            P(),
        ),
        out_specs=(P("section", None, ("dp", "round")), P("section", ("dp", "round"), None)),
        check_vma=False,
    )
```

```python
import functools

import jax
import jax.numpy as jnp
from jax import lax
from jax.experimental import pallas as pl
from jax.experimental.pallas import tpu as pltpu
from jax.sharding import PartitionSpec as P

MICRO = 1


def _recurrence_kernel(a_re_ref, a_im_ref, d_re_ref, d_im_ref, p_re_ref, p_im_ref, h_re_ref, h_im_ref, *, reverse):
    rounds, width = a_re_ref.shape
    shots = d_re_ref.shape[0]

    def step(i, carry):
        p_re, p_im, states = carry
        t = rounds - 1 - i if reverse else i
        row = pl.ds(t, 1)
        a_re = a_re_ref[row, :]
        a_im = a_im_ref[row, :]
        next_p_re = p_re * a_re - p_im * a_im
        next_p_im = p_re * a_im + p_im * a_re
        p_re_ref[row, :] = next_p_re
        p_im_ref[row, :] = next_p_im
        moved = []
        for b in range(shots):
            h_re, h_im = states[b]
            new_re = a_re * h_re - a_im * h_im + d_re_ref[b, row, :]
            new_im = a_im * h_re + a_re * h_im + d_im_ref[b, row, :]
            h_re_ref[b, row, :] = new_re
            h_im_ref[b, row, :] = new_im
            moved.append((new_re, new_im))
        return (next_p_re, next_p_im, tuple(moved))

    zero = jnp.zeros((1, width), jnp.float32)
    start = (jnp.ones((1, width), jnp.float32), zero, tuple((zero, zero) for _ in range(shots)))
    lax.fori_loop(0, rounds, step, start, unroll=8)


def recurrence(a_re, a_im, d_re, d_im, reverse=False):
    rounds, width = a_re.shape
    shots = d_re.shape[0]
    vmem = pl.BlockSpec(memory_space=pltpu.VMEM)
    coeff = jax.ShapeDtypeStruct((rounds, width), jnp.float32)
    state = jax.ShapeDtypeStruct((shots, rounds, width), jnp.float32)
    return pl.pallas_call(
        functools.partial(_recurrence_kernel, reverse=reverse),
        out_shape=(coeff, coeff, state, state),
        in_specs=[vmem] * 4,
        out_specs=(vmem,) * 4,
        cost_estimate=pl.CostEstimate(
            flops=8 * rounds * width * (shots + 1),
            transcendentals=0,
            bytes_accessed=4 * 4 * rounds * width * (shots + 1),
        ),
    )(a_re, a_im, d_re, d_im)


def entering(shard, axis, combine, identity, reverse):
    peers, position = (lax.axis_size(axis), lax.axis_index(axis))
    common = jnp.broadcast_shapes(*(part.shape for part in shard))
    stacked = jnp.stack([jnp.broadcast_to(part, common) for part in shard])
    everything = lax.all_gather(stacked, axis)
    state = tuple(
        jnp.broadcast_to(jnp.asarray(zero, part.dtype), common) for part, zero in zip(shard, identity)
    )
    for k in range(peers):
        at = peers - 1 - k if reverse else k
        reached = at > position if reverse else at < position
        new = combine(state, tuple(everything[at, i] for i in range(len(shard))))
        state = tuple(jnp.where(reached, a, b) for a, b in zip(new, state))
    return state


def ring_stage(x, axis, n, stride, dim):
    index = lax.axis_index(axis)
    size = lax.axis_size(axis)
    pos = (index // stride) % n

    def moved(j, step):
        at = (j // stride) % n
        return j - at * stride + ((at + step) % n) * stride

    ahead = [(j, moved(j, 1)) for j in range(size)]
    behind = [(j, moved(j, -1)) for j in range(size)]
    chunk = x.shape[dim] // n

    def take(part, c):
        return lax.dynamic_slice_in_dim(part, c * chunk, chunk, dim)

    first, second = x[0:1], x[1:2]
    acc_first = take(first, (pos - 1) % n)
    acc_second = take(second, (pos + 1) % n)
    for step in range(n - 1):
        acc_first = lax.ppermute(acc_first, axis, ahead) + take(first, (pos - step - 2) % n)
        acc_second = lax.ppermute(acc_second, axis, behind) + take(second, (pos + step + 2) % n)
    return jnp.concatenate([acc_first, acc_second], 0)


def reduce_scatter_rows(x):
    peers = lax.axis_size("round")
    x = ring_stage(x, "dp", lax.axis_size("dp"), 1, 1)
    split = x.reshape(x.shape[0], peers, x.shape[1] // peers, x.shape[2])
    return lax.all_to_all(split, "round", 1, 1, tiled=True).sum(axis=1)


def passed_along(value, axis, steps):
    count = lax.axis_size(axis)
    leading, last = (max(0, -steps), min(count, count - steps))
    return lax.ppermute(value, axis, [(source, source + steps) for source in range(leading, last)])


def combine_pairs(preceding, following):
    first_real, first_imag, first_state_real, first_state_imag = preceding
    second_real, second_imag, second_state_real, second_state_imag = following
    return (
        first_real * second_real - first_imag * second_imag,
        first_real * second_imag + first_imag * second_real,
        second_real * first_state_real - second_imag * first_state_imag + second_state_real,
        second_imag * first_state_real + second_real * first_state_imag + second_state_imag,
    )


def incoming_state(summary, neutral):
    return entering(summary, "round", combine_pairs, neutral, False)


def incoming_adjoint(summary, neutral):
    return entering(summary, "round", combine_pairs, neutral, True)


def neutral_of(summary):
    return (
        jnp.ones_like(summary[0]),
        jnp.zeros_like(summary[1]),
        jnp.zeros_like(summary[2]),
        jnp.zeros_like(summary[3]),
    )


def inverse_rms(values):
    return lax.rsqrt(jnp.mean(values * values, axis=-1, keepdims=True) + 1e-06)


def forward_block(inputs, weight_in, weight_out, trans_real, trans_imag, input_gain, valid_rounds):
    feature_count = inputs.shape[-1]
    widened = inputs.astype(jnp.float32)
    normed = (widened * inverse_rms(widened)).astype(jnp.bfloat16)
    driven = jnp.einsum("brw,wk->brk", normed, weight_in, preferred_element_type=jnp.float32)
    driven = driven * valid_rounds[:, :, None]
    drive_real = driven[:, :, :feature_count] * input_gain
    drive_imag = driven[:, :, feature_count:] * input_gain
    prod_real, prod_imag, local_real, local_imag = recurrence(
        trans_real, trans_imag, drive_real, drive_imag
    )
    prod_real, prod_imag = (prod_real[None], prod_imag[None])
    summary = (prod_real[:, -1], prod_imag[:, -1], local_real[:, -1], local_imag[:, -1])
    carried = incoming_state(summary, neutral_of(summary))
    carry_real = carried[2][:, None]
    carry_imag = carried[3][:, None]
    state_real = local_real + prod_real * carry_real - prod_imag * carry_imag
    state_imag = local_imag + prod_real * carry_imag + prod_imag * carry_real
    hidden = jnp.concatenate([state_real, state_imag], axis=-1).astype(jnp.bfloat16)
    mixed = jnp.einsum("brk,kw->brw", hidden, weight_out, preferred_element_type=jnp.float32)
    outputs = (widened + mixed).astype(jnp.bfloat16)
    return (outputs, normed, hidden)


def backward_block(
    inputs,
    normed,
    hidden,
    upstream,
    weight_in,
    weight_out,
    trans_real,
    trans_imag,
    input_gain,
    valid_rounds,
):
    feature_count = inputs.shape[-1]
    upstream_low = upstream.astype(jnp.bfloat16)
    grad_out = jnp.einsum("brk,brw->kw", hidden, upstream_low, preferred_element_type=jnp.float32)
    state_grad = jnp.einsum(
        "brw,kw->brk", upstream_low, weight_out, preferred_element_type=jnp.float32
    )
    error_real = state_grad[:, :, :feature_count]
    error_imag = state_grad[:, :, feature_count:]
    back_real = trans_real[None]
    back_imag = -trans_imag[None]
    pushed_real = back_real * error_real - back_imag * error_imag
    pushed_imag = back_real * error_imag + back_imag * error_real
    suffix_real, suffix_imag, local_real, local_imag = recurrence(
        back_real[0], back_imag[0], pushed_real, pushed_imag, reverse=True
    )
    suffix_real, suffix_imag = (suffix_real[None], suffix_imag[None])
    summary = (suffix_real[:, 0], suffix_imag[:, 0], local_real[:, 0], local_imag[:, 0])
    carried = incoming_adjoint(summary, neutral_of(summary))
    carry_real = carried[2][:, None]
    carry_imag = carried[3][:, None]
    passed_real = local_real + suffix_real * carry_real - suffix_imag * carry_imag
    passed_imag = local_imag + suffix_real * carry_imag + suffix_imag * carry_real
    next_real = jnp.concatenate([passed_real[:, 1:], carry_real], axis=1)
    next_imag = jnp.concatenate([passed_imag[:, 1:], carry_imag], axis=1)
    adjoint_real = error_real + next_real
    adjoint_imag = error_imag + next_imag
    drive_grad = (
        jnp.concatenate([adjoint_real * input_gain, adjoint_imag * input_gain], axis=-1)
        * valid_rounds[:, :, None]
    ).astype(jnp.bfloat16)
    grad_in = jnp.einsum("brk,brw->kw", drive_grad, normed, preferred_element_type=jnp.float32)
    normed_grad = jnp.einsum(
        "brk,wk->brw", drive_grad, weight_in, preferred_element_type=jnp.float32
    )
    widened = inputs.astype(jnp.float32)
    inv_scale = inverse_rms(widened)
    input_grad = upstream + inv_scale * (
        normed_grad
        - widened * inv_scale * inv_scale * jnp.mean(normed_grad * widened, axis=-1, keepdims=True)
    )
    return (grad_in, grad_out, input_grad)


def body(syndromes, lengths, flips, embed, w_in, w_out, leak, angle, readout):
    shots_here = syndromes.shape[0]
    rounds_here = syndromes.shape[2]
    feature_count = embed.shape[1]
    micro_shots = shots_here // MICRO
    shot_total = shots_here * lax.axis_size("dp")
    section_index = lax.axis_index("section")
    first_section = section_index == 0
    positions = lax.axis_index("round") * rounds_here + jnp.arange(rounds_here, dtype=jnp.int32)
    valid_all = (positions[None, :] < lengths[:, None]).astype(jnp.float32)
    weight_in = w_in[0]
    weight_out = w_out[0]
    forget = leak[0]
    decay_factor = jnp.exp(-forget)
    trans_real = decay_factor * jnp.cos(angle[0])[None, :]
    trans_imag = decay_factor * jnp.sin(angle[0])[None, :]
    input_gain = jnp.sqrt(-jnp.expm1(-2.0 * forget))
    readout_wide = readout.astype(jnp.float32)
    received = jnp.zeros((micro_shots, rounds_here, feature_count), jnp.bfloat16)
    saved_ticks = []
    loss_grads = []
    for tick_index in range(MICRO + 1):
        own_index = min(tick_index, MICRO - 1)
        syndrome_bits = syndromes[own_index * micro_shots : (own_index + 1) * micro_shots].astype(
            jnp.bfloat16
        )
        embedded = jnp.einsum(
            "bsr,sw->brw", syndrome_bits, embed, preferred_element_type=jnp.float32
        ).astype(jnp.bfloat16)
        inputs = jnp.where(first_section, embedded, received)
        micro_index = jnp.clip(tick_index - section_index, 0, MICRO - 1)
        valid_rounds = lax.dynamic_slice_in_dim(
            valid_all, micro_index * micro_shots, micro_shots, 0
        )
        outputs, normed, hidden = forward_block(
            inputs, weight_in, weight_out, trans_real, trans_imag, input_gain, valid_rounds
        )
        saved_ticks.append((inputs, normed, hidden, valid_rounds))
        if tick_index >= 1:
            logits = jnp.einsum("brw,w->br", outputs, readout, preferred_element_type=jnp.float32)
            targets = flips[(tick_index - 1) * micro_shots : tick_index * micro_shots].astype(
                jnp.float32
            )
            scaled = (jax.nn.sigmoid(logits) - targets) * valid_rounds / shot_total
            loss_grads.append(scaled[:, :, None] * readout_wide)
        if tick_index < MICRO:
            received = passed_along(outputs, "section", 1)
    grad_in_sum = jnp.zeros((2 * feature_count, feature_count), jnp.float32)
    grad_out_sum = jnp.zeros((2 * feature_count, feature_count), jnp.float32)
    arriving = jnp.zeros((micro_shots, rounds_here, feature_count), jnp.bfloat16)
    for tick_index in range(MICRO + 1):
        later_saved = saved_ticks[min(tick_index + 1, MICRO)]
        earlier = saved_ticks[max(tick_index - 1, 0)]
        picked = tuple(
            (jnp.where(first_section, lower, higher) for higher, lower in zip(later_saved, earlier))
        )
        own_grad = (
            loss_grads[tick_index]
            if tick_index < MICRO
            else jnp.zeros((micro_shots, rounds_here, feature_count), jnp.float32)
        )
        upstream = jnp.where(first_section, arriving.astype(jnp.float32), own_grad)
        grad_in_part, grad_out_part, input_grad = backward_block(
            picked[0],
            picked[1],
            picked[2],
            upstream,
            weight_in,
            weight_out,
            trans_real,
            trans_imag,
            input_gain,
            picked[3],
        )
        grad_in_sum = grad_in_sum + grad_in_part
        grad_out_sum = grad_out_sum + grad_out_part
        if tick_index < MICRO:
            arriving = passed_along(input_grad.astype(jnp.bfloat16), "section", -1)
    reduced = reduce_scatter_rows(jnp.stack([grad_in_sum, grad_out_sum]))
    return (jnp.swapaxes(reduced[0:1], 1, 2), reduced[1:2])


def solution(mesh):
    return jax.shard_map(
        body,
        mesh=mesh,
        in_specs=(
            P("dp", None, "round"),
            P("dp"),
            P("dp", "round"),
            P(),
            P("section", None, None),
            P("section", None, None),
            P("section", "round", None),
            P("section", None),
            P(),
        ),
        out_specs=(P("section", None, ("dp", "round")), P("section", ("dp", "round"), None)),
        check_vma=False,
    )
```

```python
import functools

import jax
import jax.numpy as jnp
from jax import lax
from jax.experimental import pallas as pl
from jax.experimental.pallas import tpu as pltpu
from jax.sharding import PartitionSpec as P

MICRO = 1


def _recurrence_kernel(
    a_re_ref, a_im_ref, d_re_ref, d_im_ref, p_re_ref, p_im_ref, h_re_ref, h_im_ref, end_ref, *, reverse
):
    rounds, width = a_re_ref.shape
    shots = d_re_ref.shape[0]

    def step(i, carry):
        p_re, p_im, states = carry
        t = rounds - 1 - i if reverse else i
        row = pl.ds(t, 1)
        a_re = a_re_ref[row, :]
        a_im = a_im_ref[row, :]
        next_p_re = p_re * a_re - p_im * a_im
        next_p_im = p_re * a_im + p_im * a_re
        p_re_ref[row, :] = next_p_re
        p_im_ref[row, :] = next_p_im
        moved = []
        for b in range(shots):
            h_re, h_im = states[b]
            new_re = a_re * h_re - a_im * h_im + d_re_ref[b, row, :]
            new_im = a_im * h_re + a_re * h_im + d_im_ref[b, row, :]
            h_re_ref[b, row, :] = new_re
            h_im_ref[b, row, :] = new_im
            moved.append((new_re, new_im))
        return (next_p_re, next_p_im, tuple(moved))

    zero = jnp.zeros((1, width), jnp.float32)
    start = (jnp.ones((1, width), jnp.float32), zero, tuple((zero, zero) for _ in range(shots)))
    p_re, p_im, states = lax.fori_loop(0, rounds, step, start, unroll=8)
    for b in range(shots):
        end_ref[0, pl.ds(b, 1), :] = p_re
        end_ref[1, pl.ds(b, 1), :] = p_im
        end_ref[2, pl.ds(b, 1), :] = states[b][0]
        end_ref[3, pl.ds(b, 1), :] = states[b][1]


def recurrence(a_re, a_im, d_re, d_im, reverse=False):
    rounds, width = a_re.shape
    shots = d_re.shape[0]
    vmem = pl.BlockSpec(memory_space=pltpu.VMEM)
    coeff = jax.ShapeDtypeStruct((rounds, width), jnp.float32)
    state = jax.ShapeDtypeStruct((shots, rounds, width), jnp.float32)
    return pl.pallas_call(
        functools.partial(_recurrence_kernel, reverse=reverse),
        out_shape=(coeff, coeff, state, state, jax.ShapeDtypeStruct((4, shots, width), jnp.float32)),
        in_specs=[vmem] * 4,
        out_specs=(vmem,) * 5,
        cost_estimate=pl.CostEstimate(
            flops=8 * rounds * width * (shots + 1),
            transcendentals=0,
            bytes_accessed=4 * 4 * rounds * width * (shots + 1),
        ),
    )(a_re, a_im, d_re, d_im)


def entering(shard, axis, combine, identity, reverse):
    peers, position = (lax.axis_size(axis), lax.axis_index(axis))
    common = jnp.broadcast_shapes(*(part.shape for part in shard))
    stacked = jnp.stack([jnp.broadcast_to(part, common) for part in shard])
    everything = lax.all_gather(stacked, axis)
    state = tuple(
        jnp.broadcast_to(jnp.asarray(zero, part.dtype), common) for part, zero in zip(shard, identity)
    )
    for k in range(peers):
        at = peers - 1 - k if reverse else k
        reached = at > position if reverse else at < position
        new = combine(state, tuple(everything[at, i] for i in range(len(shard))))
        state = tuple(jnp.where(reached, a, b) for a, b in zip(new, state))
    return state


def ring_stage(first, second, axis, n, stride, dim):
    index = lax.axis_index(axis)
    size = lax.axis_size(axis)
    pos = (index // stride) % n

    def moved(j, step):
        at = (j // stride) % n
        return j - at * stride + ((at + step) % n) * stride

    ahead = [(j, moved(j, 1)) for j in range(size)]
    behind = [(j, moved(j, -1)) for j in range(size)]
    chunk = first.shape[dim] // n

    def take(part, c):
        return lax.dynamic_slice_in_dim(part, c * chunk, chunk, dim)

    acc_first = take(first, (pos - 1) % n)
    acc_second = take(second, (pos + 1) % n)
    for step in range(n - 1):
        acc_first = lax.ppermute(acc_first, axis, ahead) + take(first, (pos - step - 2) % n)
        acc_second = lax.ppermute(acc_second, axis, behind) + take(second, (pos + step + 2) % n)
    return jnp.concatenate([acc_first, acc_second], 0)


def reduce_scatter_rows(first, second):
    peers = lax.axis_size("round")
    x = ring_stage(first, second, "dp", lax.axis_size("dp"), 1, 1)
    split = x.reshape(x.shape[0], peers, x.shape[1] // peers, x.shape[2])
    return lax.all_to_all(split, "round", 1, 1, tiled=True).sum(axis=1)


def passed_along(value, axis, steps):
    count = lax.axis_size(axis)
    leading, last = (max(0, -steps), min(count, count - steps))
    return lax.ppermute(value, axis, [(source, source + steps) for source in range(leading, last)])


def combine_pairs(preceding, following):
    first_real, first_imag, first_state_real, first_state_imag = preceding
    second_real, second_imag, second_state_real, second_state_imag = following
    return (
        first_real * second_real - first_imag * second_imag,
        first_real * second_imag + first_imag * second_real,
        second_real * first_state_real - second_imag * first_state_imag + second_state_real,
        second_imag * first_state_real + second_real * first_state_imag + second_state_imag,
    )


def incoming_state(summary, neutral):
    return entering(summary, "round", combine_pairs, neutral, False)


def incoming_adjoint(summary, neutral):
    return entering(summary, "round", combine_pairs, neutral, True)


def neutral_of(summary):
    return (
        jnp.ones_like(summary[0]),
        jnp.zeros_like(summary[1]),
        jnp.zeros_like(summary[2]),
        jnp.zeros_like(summary[3]),
    )


def inverse_rms(values):
    return lax.rsqrt(jnp.mean(values * values, axis=-1, keepdims=True) + 1e-06)


def forward_block(inputs, weight_in, weight_out, trans_real, trans_imag, input_gain, valid_rounds):
    feature_count = inputs.shape[-1]
    widened = inputs.astype(jnp.float32)
    normed = (widened * inverse_rms(widened)).astype(jnp.bfloat16)
    driven = jnp.einsum("brw,wk->brk", normed, weight_in, preferred_element_type=jnp.float32)
    driven = driven * valid_rounds[:, :, None]
    drive_real = driven[:, :, :feature_count] * input_gain
    drive_imag = driven[:, :, feature_count:] * input_gain
    prod_real, prod_imag, local_real, local_imag, ends = recurrence(
        trans_real, trans_imag, drive_real, drive_imag
    )
    prod_real, prod_imag = (prod_real[None], prod_imag[None])
    summary = (ends[0], ends[1], ends[2], ends[3])
    carried = incoming_state(summary, neutral_of(summary))
    carry_real = carried[2][:, None]
    carry_imag = carried[3][:, None]
    state_real = local_real + prod_real * carry_real - prod_imag * carry_imag
    state_imag = local_imag + prod_real * carry_imag + prod_imag * carry_real
    hidden = jnp.concatenate([state_real, state_imag], axis=-1).astype(jnp.bfloat16)
    mixed = jnp.einsum("brk,kw->brw", hidden, weight_out, preferred_element_type=jnp.float32)
    outputs = (widened + mixed).astype(jnp.bfloat16)
    return (outputs, normed, hidden)


def backward_block(
    inputs,
    normed,
    hidden,
    upstream,
    weight_in,
    weight_out,
    trans_real,
    trans_imag,
    input_gain,
    valid_rounds,
):
    feature_count = inputs.shape[-1]
    upstream_low = upstream.astype(jnp.bfloat16)
    grad_out = jnp.einsum("brk,brw->kw", hidden, upstream_low, preferred_element_type=jnp.float32)
    state_grad = jnp.einsum(
        "brw,kw->brk", upstream_low, weight_out, preferred_element_type=jnp.float32
    )
    error_real = state_grad[:, :, :feature_count]
    error_imag = state_grad[:, :, feature_count:]
    back_real = trans_real[None]
    back_imag = -trans_imag[None]
    pushed_real = back_real * error_real - back_imag * error_imag
    pushed_imag = back_real * error_imag + back_imag * error_real
    suffix_real, suffix_imag, local_real, local_imag, ends = recurrence(
        back_real[0], back_imag[0], pushed_real, pushed_imag, reverse=True
    )
    suffix_real, suffix_imag = (suffix_real[None], suffix_imag[None])
    summary = (ends[0], ends[1], ends[2], ends[3])
    carried = incoming_adjoint(summary, neutral_of(summary))
    carry_real = carried[2][:, None]
    carry_imag = carried[3][:, None]
    passed_real = local_real + suffix_real * carry_real - suffix_imag * carry_imag
    passed_imag = local_imag + suffix_real * carry_imag + suffix_imag * carry_real
    next_real = jnp.concatenate([passed_real[:, 1:], carry_real], axis=1)
    next_imag = jnp.concatenate([passed_imag[:, 1:], carry_imag], axis=1)
    adjoint_real = error_real + next_real
    adjoint_imag = error_imag + next_imag
    drive_grad = (
        jnp.concatenate([adjoint_real * input_gain, adjoint_imag * input_gain], axis=-1)
        * valid_rounds[:, :, None]
    ).astype(jnp.bfloat16)
    grad_in = jnp.einsum("brk,brw->kw", drive_grad, normed, preferred_element_type=jnp.float32)
    normed_grad = jnp.einsum(
        "brk,wk->brw", drive_grad, weight_in, preferred_element_type=jnp.float32
    )
    widened = inputs.astype(jnp.float32)
    inv_scale = inverse_rms(widened)
    input_grad = upstream + inv_scale * (
        normed_grad
        - widened * inv_scale * inv_scale * jnp.mean(normed_grad * widened, axis=-1, keepdims=True)
    )
    return (grad_in, grad_out, input_grad)


def body(syndromes, lengths, flips, embed, w_in, w_out, leak, angle, readout):
    shots_here = syndromes.shape[0]
    rounds_here = syndromes.shape[2]
    feature_count = embed.shape[1]
    micro_shots = shots_here // MICRO
    shot_total = shots_here * lax.axis_size("dp")
    section_index = lax.axis_index("section")
    first_section = section_index == 0
    positions = lax.axis_index("round") * rounds_here + jnp.arange(rounds_here, dtype=jnp.int32)
    valid_all = (positions[None, :] < lengths[:, None]).astype(jnp.float32)
    weight_in = w_in[0]
    weight_out = w_out[0]
    forget = leak[0]
    decay_factor = jnp.exp(-forget)
    trans_real = decay_factor * jnp.cos(angle[0])[None, :]
    trans_imag = decay_factor * jnp.sin(angle[0])[None, :]
    input_gain = jnp.sqrt(-jnp.expm1(-2.0 * forget))
    readout_wide = readout.astype(jnp.float32)
    received = jnp.zeros((micro_shots, rounds_here, feature_count), jnp.bfloat16)
    saved_ticks = []
    loss_grads = []
    for tick_index in range(MICRO + 1):
        own_index = min(tick_index, MICRO - 1)
        syndrome_bits = syndromes[own_index * micro_shots : (own_index + 1) * micro_shots].astype(
            jnp.bfloat16
        )
        embedded = jnp.einsum(
            "bsr,sw->brw", syndrome_bits, embed, preferred_element_type=jnp.float32
        ).astype(jnp.bfloat16)
        inputs = jnp.where(first_section, embedded, received)
        micro_index = jnp.clip(tick_index - section_index, 0, MICRO - 1)
        valid_rounds = lax.dynamic_slice_in_dim(
            valid_all, micro_index * micro_shots, micro_shots, 0
        )
        outputs, normed, hidden = forward_block(
            inputs, weight_in, weight_out, trans_real, trans_imag, input_gain, valid_rounds
        )
        saved_ticks.append((inputs, normed, hidden, valid_rounds))
        if tick_index >= 1:
            logits = jnp.einsum("brw,w->br", outputs, readout, preferred_element_type=jnp.float32)
            targets = flips[(tick_index - 1) * micro_shots : tick_index * micro_shots].astype(
                jnp.float32
            )
            scaled = (jax.nn.sigmoid(logits) - targets) * valid_rounds / shot_total
            loss_grads.append(scaled[:, :, None] * readout_wide)
        if tick_index < MICRO:
            received = passed_along(outputs, "section", 1)
    grad_in_sum = jnp.zeros((2 * feature_count, feature_count), jnp.float32)
    grad_out_sum = jnp.zeros((2 * feature_count, feature_count), jnp.float32)
    arriving = jnp.zeros((micro_shots, rounds_here, feature_count), jnp.bfloat16)
    for tick_index in range(MICRO + 1):
        later_saved = saved_ticks[min(tick_index + 1, MICRO)]
        earlier = saved_ticks[max(tick_index - 1, 0)]
        picked = tuple(
            (jnp.where(first_section, lower, higher) for higher, lower in zip(later_saved, earlier))
        )
        own_grad = (
            loss_grads[tick_index]
            if tick_index < MICRO
            else jnp.zeros((micro_shots, rounds_here, feature_count), jnp.float32)
        )
        upstream = jnp.where(first_section, arriving.astype(jnp.float32), own_grad)
        grad_in_part, grad_out_part, input_grad = backward_block(
            picked[0],
            picked[1],
            picked[2],
            upstream,
            weight_in,
            weight_out,
            trans_real,
            trans_imag,
            input_gain,
            picked[3],
        )
        grad_in_sum = grad_in_sum + grad_in_part
        grad_out_sum = grad_out_sum + grad_out_part
        if tick_index < MICRO:
            arriving = passed_along(input_grad.astype(jnp.bfloat16), "section", -1)
    reduced = reduce_scatter_rows(grad_in_sum[None], grad_out_sum[None])
    return (jnp.swapaxes(reduced[0:1], 1, 2), reduced[1:2])


def solution(mesh):
    return jax.shard_map(
        body,
        mesh=mesh,
        in_specs=(
            P("dp", None, "round"),
            P("dp"),
            P("dp", "round"),
            P(),
            P("section", None, None),
            P("section", None, None),
            P("section", "round", None),
            P("section", None),
            P(),
        ),
        out_specs=(P("section", None, ("dp", "round")), P("section", ("dp", "round"), None)),
        check_vma=False,
    )
```

```python
import functools

import jax
import jax.numpy as jnp
from jax import lax
from jax.experimental import pallas as pl
from jax.experimental.pallas import tpu as pltpu
from jax.sharding import PartitionSpec as P

MICRO = 1


def _recurrence_kernel(
    a_re_ref, a_im_ref, d_re_ref, d_im_ref, p_re_ref, p_im_ref, h_re_ref, h_im_ref, end_ref, *, reverse
):
    rounds, width = a_re_ref.shape
    shots = d_re_ref.shape[0]

    def step(i, carry):
        p_re, p_im, states = carry
        t = rounds - 1 - i if reverse else i
        row = pl.ds(t, 1)
        a_re = a_re_ref[row, :]
        a_im = a_im_ref[row, :]
        next_p_re = p_re * a_re - p_im * a_im
        next_p_im = p_re * a_im + p_im * a_re
        p_re_ref[row, :] = next_p_re
        p_im_ref[row, :] = next_p_im
        moved = []
        for b in range(shots):
            h_re, h_im = states[b]
            new_re = a_re * h_re - a_im * h_im + d_re_ref[b, row, :]
            new_im = a_im * h_re + a_re * h_im + d_im_ref[b, row, :]
            h_re_ref[b, row, :] = new_re
            h_im_ref[b, row, :] = new_im
            moved.append((new_re, new_im))
        return (next_p_re, next_p_im, tuple(moved))

    zero = jnp.zeros((1, width), jnp.float32)
    start = (jnp.ones((1, width), jnp.float32), zero, tuple((zero, zero) for _ in range(shots)))
    p_re, p_im, states = lax.fori_loop(0, rounds, step, start, unroll=8)
    for b in range(shots):
        end_ref[0, pl.ds(b, 1), :] = p_re
        end_ref[1, pl.ds(b, 1), :] = p_im
        end_ref[2, pl.ds(b, 1), :] = states[b][0]
        end_ref[3, pl.ds(b, 1), :] = states[b][1]


def recurrence(a_re, a_im, d_re, d_im, reverse=False):
    rounds, width = a_re.shape
    shots = d_re.shape[0]
    vmem = pl.BlockSpec(memory_space=pltpu.VMEM)
    coeff = jax.ShapeDtypeStruct((rounds, width), jnp.float32)
    state = jax.ShapeDtypeStruct((shots, rounds, width), jnp.float32)
    return pl.pallas_call(
        functools.partial(_recurrence_kernel, reverse=reverse),
        out_shape=(coeff, coeff, state, state, jax.ShapeDtypeStruct((4, shots, width), jnp.float32)),
        in_specs=[vmem] * 4,
        out_specs=(vmem,) * 5,
        cost_estimate=pl.CostEstimate(
            flops=8 * rounds * width * (shots + 1),
            transcendentals=0,
            bytes_accessed=4 * 4 * rounds * width * (shots + 1),
        ),
    )(a_re, a_im, d_re, d_im)


def entering(shard, axis, combine, identity, reverse):
    peers, position = (lax.axis_size(axis), lax.axis_index(axis))
    common = jnp.broadcast_shapes(*(part.shape for part in shard))
    stacked = jnp.stack([jnp.broadcast_to(part, common) for part in shard])
    copies = jnp.broadcast_to(stacked[None], (peers,) + stacked.shape)
    everything = lax.all_to_all(copies, axis, 0, 0, tiled=True)
    state = tuple(
        jnp.broadcast_to(jnp.asarray(zero, part.dtype), common) for part, zero in zip(shard, identity)
    )
    for k in range(peers):
        at = peers - 1 - k if reverse else k
        reached = at > position if reverse else at < position
        new = combine(state, tuple(everything[at, i] for i in range(len(shard))))
        state = tuple(jnp.where(reached, a, b) for a, b in zip(new, state))
    return state


def ring_stage(first, second, axis, n, stride, dim):
    index = lax.axis_index(axis)
    size = lax.axis_size(axis)
    pos = (index // stride) % n

    def moved(j, step):
        at = (j // stride) % n
        return j - at * stride + ((at + step) % n) * stride

    ahead = [(j, moved(j, 1)) for j in range(size)]
    behind = [(j, moved(j, -1)) for j in range(size)]
    chunk = first.shape[dim] // n

    def take(part, c):
        return lax.dynamic_slice_in_dim(part, c * chunk, chunk, dim)

    acc_first = take(first, (pos - 1) % n)
    acc_second = take(second, (pos + 1) % n)
    for step in range(n - 1):
        acc_first = lax.ppermute(acc_first, axis, ahead) + take(first, (pos - step - 2) % n)
        acc_second = lax.ppermute(acc_second, axis, behind) + take(second, (pos + step + 2) % n)
    return jnp.concatenate([acc_first, acc_second], 0)


def reduce_scatter_rows(first, second):
    peers = lax.axis_size("round")
    x = ring_stage(first, second, "dp", lax.axis_size("dp"), 1, 1)
    split = x.reshape(x.shape[0], peers, x.shape[1] // peers, x.shape[2])
    return lax.all_to_all(split, "round", 1, 1, tiled=True).sum(axis=1)


def passed_along(value, axis, steps):
    count = lax.axis_size(axis)
    leading, last = (max(0, -steps), min(count, count - steps))
    return lax.ppermute(value, axis, [(source, source + steps) for source in range(leading, last)])


def combine_pairs(preceding, following):
    first_real, first_imag, first_state_real, first_state_imag = preceding
    second_real, second_imag, second_state_real, second_state_imag = following
    return (
        first_real * second_real - first_imag * second_imag,
        first_real * second_imag + first_imag * second_real,
        second_real * first_state_real - second_imag * first_state_imag + second_state_real,
        second_imag * first_state_real + second_real * first_state_imag + second_state_imag,
    )


def incoming_state(summary, neutral):
    return entering(summary, "round", combine_pairs, neutral, False)


def incoming_adjoint(summary, neutral):
    return entering(summary, "round", combine_pairs, neutral, True)


def neutral_of(summary):
    return (
        jnp.ones_like(summary[0]),
        jnp.zeros_like(summary[1]),
        jnp.zeros_like(summary[2]),
        jnp.zeros_like(summary[3]),
    )


def inverse_rms(values):
    return lax.rsqrt(jnp.mean(values * values, axis=-1, keepdims=True) + 1e-06)


def forward_block(inputs, weight_in, weight_out, trans_real, trans_imag, input_gain, valid_rounds):
    feature_count = inputs.shape[-1]
    widened = inputs.astype(jnp.float32)
    normed = (widened * inverse_rms(widened)).astype(jnp.bfloat16)
    driven = jnp.einsum("brw,wk->brk", normed, weight_in, preferred_element_type=jnp.float32)
    driven = driven * valid_rounds[:, :, None]
    drive_real = driven[:, :, :feature_count] * input_gain
    drive_imag = driven[:, :, feature_count:] * input_gain
    prod_real, prod_imag, local_real, local_imag, ends = recurrence(
        trans_real, trans_imag, drive_real, drive_imag
    )
    prod_real, prod_imag = (prod_real[None], prod_imag[None])
    summary = (ends[0], ends[1], ends[2], ends[3])
    carried = incoming_state(summary, neutral_of(summary))
    carry_real = carried[2][:, None]
    carry_imag = carried[3][:, None]
    state_real = local_real + prod_real * carry_real - prod_imag * carry_imag
    state_imag = local_imag + prod_real * carry_imag + prod_imag * carry_real
    hidden = jnp.concatenate([state_real, state_imag], axis=-1).astype(jnp.bfloat16)
    mixed = jnp.einsum("brk,kw->brw", hidden, weight_out, preferred_element_type=jnp.float32)
    outputs = (widened + mixed).astype(jnp.bfloat16)
    return (outputs, normed, hidden)


def backward_block(
    inputs,
    normed,
    hidden,
    upstream,
    weight_in,
    weight_out,
    trans_real,
    trans_imag,
    input_gain,
    valid_rounds,
):
    feature_count = inputs.shape[-1]
    upstream_low = upstream.astype(jnp.bfloat16)
    grad_out = jnp.einsum("brk,brw->kw", hidden, upstream_low, preferred_element_type=jnp.float32)
    state_grad = jnp.einsum(
        "brw,kw->brk", upstream_low, weight_out, preferred_element_type=jnp.float32
    )
    error_real = state_grad[:, :, :feature_count]
    error_imag = state_grad[:, :, feature_count:]
    back_real = trans_real[None]
    back_imag = -trans_imag[None]
    pushed_real = back_real * error_real - back_imag * error_imag
    pushed_imag = back_real * error_imag + back_imag * error_real
    suffix_real, suffix_imag, local_real, local_imag, ends = recurrence(
        back_real[0], back_imag[0], pushed_real, pushed_imag, reverse=True
    )
    suffix_real, suffix_imag = (suffix_real[None], suffix_imag[None])
    summary = (ends[0], ends[1], ends[2], ends[3])
    carried = incoming_adjoint(summary, neutral_of(summary))
    carry_real = carried[2][:, None]
    carry_imag = carried[3][:, None]
    passed_real = local_real + suffix_real * carry_real - suffix_imag * carry_imag
    passed_imag = local_imag + suffix_real * carry_imag + suffix_imag * carry_real
    next_real = jnp.concatenate([passed_real[:, 1:], carry_real], axis=1)
    next_imag = jnp.concatenate([passed_imag[:, 1:], carry_imag], axis=1)
    adjoint_real = error_real + next_real
    adjoint_imag = error_imag + next_imag
    drive_grad = (
        jnp.concatenate([adjoint_real * input_gain, adjoint_imag * input_gain], axis=-1)
        * valid_rounds[:, :, None]
    ).astype(jnp.bfloat16)
    grad_in = jnp.einsum("brk,brw->kw", drive_grad, normed, preferred_element_type=jnp.float32)
    normed_grad = jnp.einsum(
        "brk,wk->brw", drive_grad, weight_in, preferred_element_type=jnp.float32
    )
    widened = inputs.astype(jnp.float32)
    inv_scale = inverse_rms(widened)
    input_grad = upstream + inv_scale * (
        normed_grad
        - widened * inv_scale * inv_scale * jnp.mean(normed_grad * widened, axis=-1, keepdims=True)
    )
    return (grad_in, grad_out, input_grad)


def body(syndromes, lengths, flips, embed, w_in, w_out, leak, angle, readout):
    shots_here = syndromes.shape[0]
    rounds_here = syndromes.shape[2]
    feature_count = embed.shape[1]
    micro_shots = shots_here // MICRO
    shot_total = shots_here * lax.axis_size("dp")
    section_index = lax.axis_index("section")
    first_section = section_index == 0
    positions = lax.axis_index("round") * rounds_here + jnp.arange(rounds_here, dtype=jnp.int32)
    valid_all = (positions[None, :] < lengths[:, None]).astype(jnp.float32)
    weight_in = w_in[0]
    weight_out = w_out[0]
    forget = leak[0]
    decay_factor = jnp.exp(-forget)
    trans_real = decay_factor * jnp.cos(angle[0])[None, :]
    trans_imag = decay_factor * jnp.sin(angle[0])[None, :]
    input_gain = jnp.sqrt(-jnp.expm1(-2.0 * forget))
    readout_wide = readout.astype(jnp.float32)
    received = jnp.zeros((micro_shots, rounds_here, feature_count), jnp.bfloat16)
    saved_ticks = []
    loss_grads = []
    for tick_index in range(MICRO + 1):
        own_index = min(tick_index, MICRO - 1)
        syndrome_bits = syndromes[own_index * micro_shots : (own_index + 1) * micro_shots].astype(
            jnp.bfloat16
        )
        embedded = jnp.einsum(
            "bsr,sw->brw", syndrome_bits, embed, preferred_element_type=jnp.float32
        ).astype(jnp.bfloat16)
        inputs = jnp.where(first_section, embedded, received)
        micro_index = jnp.clip(tick_index - section_index, 0, MICRO - 1)
        valid_rounds = lax.dynamic_slice_in_dim(
            valid_all, micro_index * micro_shots, micro_shots, 0
        )
        outputs, normed, hidden = forward_block(
            inputs, weight_in, weight_out, trans_real, trans_imag, input_gain, valid_rounds
        )
        saved_ticks.append((inputs, normed, hidden, valid_rounds))
        if tick_index >= 1:
            logits = jnp.einsum("brw,w->br", outputs, readout, preferred_element_type=jnp.float32)
            targets = flips[(tick_index - 1) * micro_shots : tick_index * micro_shots].astype(
                jnp.float32
            )
            scaled = (jax.nn.sigmoid(logits) - targets) * valid_rounds / shot_total
            loss_grads.append(scaled[:, :, None] * readout_wide)
        if tick_index < MICRO:
            received = passed_along(outputs, "section", 1)
    grad_in_sum = jnp.zeros((2 * feature_count, feature_count), jnp.float32)
    grad_out_sum = jnp.zeros((2 * feature_count, feature_count), jnp.float32)
    arriving = jnp.zeros((micro_shots, rounds_here, feature_count), jnp.bfloat16)
    for tick_index in range(MICRO + 1):
        later_saved = saved_ticks[min(tick_index + 1, MICRO)]
        earlier = saved_ticks[max(tick_index - 1, 0)]
        picked = tuple(
            (jnp.where(first_section, lower, higher) for higher, lower in zip(later_saved, earlier))
        )
        own_grad = (
            loss_grads[tick_index]
            if tick_index < MICRO
            else jnp.zeros((micro_shots, rounds_here, feature_count), jnp.float32)
        )
        upstream = jnp.where(first_section, arriving.astype(jnp.float32), own_grad)
        grad_in_part, grad_out_part, input_grad = backward_block(
            picked[0],
            picked[1],
            picked[2],
            upstream,
            weight_in,
            weight_out,
            trans_real,
            trans_imag,
            input_gain,
            picked[3],
        )
        grad_in_sum = grad_in_sum + grad_in_part
        grad_out_sum = grad_out_sum + grad_out_part
        if tick_index < MICRO:
            arriving = passed_along(input_grad.astype(jnp.bfloat16), "section", -1)
    reduced = reduce_scatter_rows(grad_in_sum[None], grad_out_sum[None])
    return (jnp.swapaxes(reduced[0:1], 1, 2), reduced[1:2])


def solution(mesh):
    return jax.shard_map(
        body,
        mesh=mesh,
        in_specs=(
            P("dp", None, "round"),
            P("dp"),
            P("dp", "round"),
            P(),
            P("section", None, None),
            P("section", None, None),
            P("section", "round", None),
            P("section", None),
            P(),
        ),
        out_specs=(P("section", None, ("dp", "round")), P("section", ("dp", "round"), None)),
        check_vma=False,
    )
```

```python
import functools

import jax
import jax.numpy as jnp
from jax import lax
from jax.experimental import pallas as pl
from jax.experimental.pallas import tpu as pltpu
from jax.sharding import PartitionSpec as P

MICRO = 1


def _recurrence_kernel(
    a_re_ref, a_im_ref, d_re_ref, d_im_ref, p_re_ref, p_im_ref, h_re_ref, h_im_ref, end_ref, *, reverse
):
    rounds, width = a_re_ref.shape
    shots = d_re_ref.shape[0]

    def step(i, carry):
        p_re, p_im, states = carry
        t = rounds - 1 - i if reverse else i
        row = pl.ds(t, 1)
        a_re = a_re_ref[row, :]
        a_im = a_im_ref[row, :]
        next_p_re = p_re * a_re - p_im * a_im
        next_p_im = p_re * a_im + p_im * a_re
        p_re_ref[row, :] = next_p_re
        p_im_ref[row, :] = next_p_im
        moved = []
        for b in range(shots):
            h_re, h_im = states[b]
            new_re = a_re * h_re - a_im * h_im + d_re_ref[b, row, :]
            new_im = a_im * h_re + a_re * h_im + d_im_ref[b, row, :]
            h_re_ref[b, row, :] = new_re
            h_im_ref[b, row, :] = new_im
            moved.append((new_re, new_im))
        return (next_p_re, next_p_im, tuple(moved))

    zero = jnp.zeros((1, width), jnp.float32)
    start = (jnp.ones((1, width), jnp.float32), zero, tuple((zero, zero) for _ in range(shots)))
    p_re, p_im, states = lax.fori_loop(0, rounds, step, start, unroll=8)
    for b in range(shots):
        end_ref[0, pl.ds(b, 1), :] = p_re
        end_ref[1, pl.ds(b, 1), :] = p_im
        end_ref[2, pl.ds(b, 1), :] = states[b][0]
        end_ref[3, pl.ds(b, 1), :] = states[b][1]


def recurrence(a_re, a_im, d_re, d_im, reverse=False):
    rounds, width = a_re.shape
    shots = d_re.shape[0]
    vmem = pl.BlockSpec(memory_space=pltpu.VMEM)
    coeff = jax.ShapeDtypeStruct((rounds, width), jnp.float32)
    state = jax.ShapeDtypeStruct((shots, rounds, width), jnp.float32)
    return pl.pallas_call(
        functools.partial(_recurrence_kernel, reverse=reverse),
        out_shape=(coeff, coeff, state, state, jax.ShapeDtypeStruct((4, shots, width), jnp.float32)),
        in_specs=[vmem] * 4,
        out_specs=(vmem,) * 5,
        cost_estimate=pl.CostEstimate(
            flops=8 * rounds * width * (shots + 1),
            transcendentals=0,
            bytes_accessed=4 * 4 * rounds * width * (shots + 1),
        ),
    )(a_re, a_im, d_re, d_im)


def entering(shard, axis, combine, identity, reverse):
    peers, position = (lax.axis_size(axis), lax.axis_index(axis))
    common = jnp.broadcast_shapes(*(part.shape for part in shard))
    stacked = jnp.stack([jnp.broadcast_to(part, common) for part in shard])
    copies = jnp.broadcast_to(stacked[None], (peers,) + stacked.shape)
    everything = lax.all_to_all(copies, axis, 0, 0, tiled=True)
    state = tuple(
        jnp.broadcast_to(jnp.asarray(zero, part.dtype), common) for part, zero in zip(shard, identity)
    )
    for k in range(peers):
        at = peers - 1 - k if reverse else k
        reached = at > position if reverse else at < position
        new = combine(state, tuple(everything[at, i] for i in range(len(shard))))
        state = tuple(jnp.where(reached, a, b) for a, b in zip(new, state))
    return state


def ring_stage(first, second, axis, n, stride, dim):
    index = lax.axis_index(axis)
    size = lax.axis_size(axis)
    pos = (index // stride) % n

    def moved(j, step):
        at = (j // stride) % n
        return j - at * stride + ((at + step) % n) * stride

    ahead = [(j, moved(j, 1)) for j in range(size)]
    behind = [(j, moved(j, -1)) for j in range(size)]
    chunk = first.shape[dim] // n

    def take(part, c):
        return lax.dynamic_slice_in_dim(part, c * chunk, chunk, dim)

    acc_first = take(first, (pos - 1) % n)
    acc_second = take(second, (pos + 1) % n)
    for step in range(n - 1):
        acc_first = lax.ppermute(acc_first, axis, ahead) + take(first, (pos - step - 2) % n)
        acc_second = lax.ppermute(acc_second, axis, behind) + take(second, (pos + step + 2) % n)
    return jnp.concatenate([acc_first, acc_second], 0)


def reduce_scatter_rows(first, second):
    peers = lax.axis_size("round")
    groups = lax.axis_size("dp")
    rows, width = first.shape[1], first.shape[2]
    half = width // 2
    early = second.reshape(1, groups, peers, rows // (groups * peers), width)
    early = lax.all_to_all(early, "round", 2, 2, tiled=True).sum(axis=2)
    early = early.reshape(1, rows // peers, width)
    early = ring_stage(early[..., :half], early[..., half:], "dp", groups, 1, 1)
    late = ring_stage(first[..., :half], first[..., half:], "dp", groups, 1, 1)
    late = jnp.concatenate([late[0:1], late[1:2]], axis=2)
    late = late.reshape(1, peers, late.shape[1] // peers, width)
    late = lax.all_to_all(late, "round", 1, 1, tiled=True).sum(axis=1)
    return jnp.concatenate([late, jnp.concatenate([early[0:1], early[1:2]], axis=2)], 0)


def passed_along(value, axis, steps):
    count = lax.axis_size(axis)
    leading, last = (max(0, -steps), min(count, count - steps))
    return lax.ppermute(value, axis, [(source, source + steps) for source in range(leading, last)])


def combine_pairs(preceding, following):
    first_real, first_imag, first_state_real, first_state_imag = preceding
    second_real, second_imag, second_state_real, second_state_imag = following
    return (
        first_real * second_real - first_imag * second_imag,
        first_real * second_imag + first_imag * second_real,
        second_real * first_state_real - second_imag * first_state_imag + second_state_real,
        second_imag * first_state_real + second_real * first_state_imag + second_state_imag,
    )


def incoming_state(summary, neutral):
    return entering(summary, "round", combine_pairs, neutral, False)


def incoming_adjoint(summary, neutral):
    return entering(summary, "round", combine_pairs, neutral, True)


def neutral_of(summary):
    return (
        jnp.ones_like(summary[0]),
        jnp.zeros_like(summary[1]),
        jnp.zeros_like(summary[2]),
        jnp.zeros_like(summary[3]),
    )


def inverse_rms(values):
    return lax.rsqrt(jnp.mean(values * values, axis=-1, keepdims=True) + 1e-06)


def forward_block(inputs, weight_in, weight_out, trans_real, trans_imag, input_gain, valid_rounds):
    feature_count = inputs.shape[-1]
    widened = inputs.astype(jnp.float32)
    normed = (widened * inverse_rms(widened)).astype(jnp.bfloat16)
    driven = jnp.einsum("brw,wk->brk", normed, weight_in, preferred_element_type=jnp.float32)
    driven = driven * valid_rounds[:, :, None]
    drive_real = driven[:, :, :feature_count] * input_gain
    drive_imag = driven[:, :, feature_count:] * input_gain
    prod_real, prod_imag, local_real, local_imag, ends = recurrence(
        trans_real, trans_imag, drive_real, drive_imag
    )
    prod_real, prod_imag = (prod_real[None], prod_imag[None])
    summary = (ends[0], ends[1], ends[2], ends[3])
    carried = incoming_state(summary, neutral_of(summary))
    carry_real = carried[2][:, None]
    carry_imag = carried[3][:, None]
    state_real = local_real + prod_real * carry_real - prod_imag * carry_imag
    state_imag = local_imag + prod_real * carry_imag + prod_imag * carry_real
    hidden = jnp.concatenate([state_real, state_imag], axis=-1).astype(jnp.bfloat16)
    mixed = jnp.einsum("brk,kw->brw", hidden, weight_out, preferred_element_type=jnp.float32)
    outputs = (widened + mixed).astype(jnp.bfloat16)
    return (outputs, normed, hidden)


def backward_block(
    inputs,
    normed,
    hidden,
    upstream,
    weight_in,
    weight_out,
    trans_real,
    trans_imag,
    input_gain,
    valid_rounds,
):
    feature_count = inputs.shape[-1]
    upstream_low = upstream.astype(jnp.bfloat16)
    grad_out = jnp.einsum("brk,brw->kw", hidden, upstream_low, preferred_element_type=jnp.float32)
    state_grad = jnp.einsum(
        "brw,kw->brk", upstream_low, weight_out, preferred_element_type=jnp.float32
    )
    error_real = state_grad[:, :, :feature_count]
    error_imag = state_grad[:, :, feature_count:]
    back_real = trans_real[None]
    back_imag = -trans_imag[None]
    pushed_real = back_real * error_real - back_imag * error_imag
    pushed_imag = back_real * error_imag + back_imag * error_real
    suffix_real, suffix_imag, local_real, local_imag, ends = recurrence(
        back_real[0], back_imag[0], pushed_real, pushed_imag, reverse=True
    )
    suffix_real, suffix_imag = (suffix_real[None], suffix_imag[None])
    summary = (ends[0], ends[1], ends[2], ends[3])
    carried = incoming_adjoint(summary, neutral_of(summary))
    carry_real = carried[2][:, None]
    carry_imag = carried[3][:, None]
    passed_real = local_real + suffix_real * carry_real - suffix_imag * carry_imag
    passed_imag = local_imag + suffix_real * carry_imag + suffix_imag * carry_real
    next_real = jnp.concatenate([passed_real[:, 1:], carry_real], axis=1)
    next_imag = jnp.concatenate([passed_imag[:, 1:], carry_imag], axis=1)
    adjoint_real = error_real + next_real
    adjoint_imag = error_imag + next_imag
    drive_grad = (
        jnp.concatenate([adjoint_real * input_gain, adjoint_imag * input_gain], axis=-1)
        * valid_rounds[:, :, None]
    ).astype(jnp.bfloat16)
    grad_in = jnp.einsum("brk,brw->kw", drive_grad, normed, preferred_element_type=jnp.float32)
    normed_grad = jnp.einsum(
        "brk,wk->brw", drive_grad, weight_in, preferred_element_type=jnp.float32
    )
    widened = inputs.astype(jnp.float32)
    inv_scale = inverse_rms(widened)
    input_grad = upstream + inv_scale * (
        normed_grad
        - widened * inv_scale * inv_scale * jnp.mean(normed_grad * widened, axis=-1, keepdims=True)
    )
    return (grad_in, grad_out, input_grad)


def body(syndromes, lengths, flips, embed, w_in, w_out, leak, angle, readout):
    shots_here = syndromes.shape[0]
    rounds_here = syndromes.shape[2]
    feature_count = embed.shape[1]
    micro_shots = shots_here // MICRO
    shot_total = shots_here * lax.axis_size("dp")
    section_index = lax.axis_index("section")
    first_section = section_index == 0
    positions = lax.axis_index("round") * rounds_here + jnp.arange(rounds_here, dtype=jnp.int32)
    valid_all = (positions[None, :] < lengths[:, None]).astype(jnp.float32)
    weight_in = w_in[0]
    weight_out = w_out[0]
    forget = leak[0]
    decay_factor = jnp.exp(-forget)
    trans_real = decay_factor * jnp.cos(angle[0])[None, :]
    trans_imag = decay_factor * jnp.sin(angle[0])[None, :]
    input_gain = jnp.sqrt(-jnp.expm1(-2.0 * forget))
    readout_wide = readout.astype(jnp.float32)
    received = jnp.zeros((micro_shots, rounds_here, feature_count), jnp.bfloat16)
    saved_ticks = []
    loss_grads = []
    for tick_index in range(MICRO + 1):
        own_index = min(tick_index, MICRO - 1)
        syndrome_bits = syndromes[own_index * micro_shots : (own_index + 1) * micro_shots].astype(
            jnp.bfloat16
        )
        embedded = jnp.einsum(
            "bsr,sw->brw", syndrome_bits, embed, preferred_element_type=jnp.float32
        ).astype(jnp.bfloat16)
        inputs = jnp.where(first_section, embedded, received)
        micro_index = jnp.clip(tick_index - section_index, 0, MICRO - 1)
        valid_rounds = lax.dynamic_slice_in_dim(
            valid_all, micro_index * micro_shots, micro_shots, 0
        )
        outputs, normed, hidden = forward_block(
            inputs, weight_in, weight_out, trans_real, trans_imag, input_gain, valid_rounds
        )
        saved_ticks.append((inputs, normed, hidden, valid_rounds))
        if tick_index >= 1:
            logits = jnp.einsum("brw,w->br", outputs, readout, preferred_element_type=jnp.float32)
            targets = flips[(tick_index - 1) * micro_shots : tick_index * micro_shots].astype(
                jnp.float32
            )
            scaled = (jax.nn.sigmoid(logits) - targets) * valid_rounds / shot_total
            loss_grads.append(scaled[:, :, None] * readout_wide)
        if tick_index < MICRO:
            received = passed_along(outputs, "section", 1)
    grad_in_sum = jnp.zeros((2 * feature_count, feature_count), jnp.float32)
    grad_out_sum = jnp.zeros((2 * feature_count, feature_count), jnp.float32)
    arriving = jnp.zeros((micro_shots, rounds_here, feature_count), jnp.bfloat16)
    for tick_index in range(MICRO + 1):
        later_saved = saved_ticks[min(tick_index + 1, MICRO)]
        earlier = saved_ticks[max(tick_index - 1, 0)]
        picked = tuple(
            (jnp.where(first_section, lower, higher) for higher, lower in zip(later_saved, earlier))
        )
        own_grad = (
            loss_grads[tick_index]
            if tick_index < MICRO
            else jnp.zeros((micro_shots, rounds_here, feature_count), jnp.float32)
        )
        upstream = jnp.where(first_section, arriving.astype(jnp.float32), own_grad)
        grad_in_part, grad_out_part, input_grad = backward_block(
            picked[0],
            picked[1],
            picked[2],
            upstream,
            weight_in,
            weight_out,
            trans_real,
            trans_imag,
            input_gain,
            picked[3],
        )
        grad_in_sum = grad_in_sum + grad_in_part
        grad_out_sum = grad_out_sum + grad_out_part
        if tick_index < MICRO:
            arriving = passed_along(input_grad.astype(jnp.bfloat16), "section", -1)
    reduced = reduce_scatter_rows(grad_in_sum[None], grad_out_sum[None])
    return (jnp.swapaxes(reduced[0:1], 1, 2), reduced[1:2])


def solution(mesh):
    return jax.shard_map(
        body,
        mesh=mesh,
        in_specs=(
            P("dp", None, "round"),
            P("dp"),
            P("dp", "round"),
            P(),
            P("section", None, None),
            P("section", None, None),
            P("section", "round", None),
            P("section", None),
            P(),
        ),
        out_specs=(P("section", None, ("dp", "round")), P("section", ("dp", "round"), None)),
        check_vma=False,
    )
```

```python
import functools

import jax
import jax.numpy as jnp
from jax import lax
from jax.experimental import pallas as pl
from jax.experimental.pallas import tpu as pltpu
from jax.sharding import PartitionSpec as P

MICRO = 1


def _recurrence_kernel(
    a_re_ref, a_im_ref, d_re_ref, d_im_ref, p_re_ref, p_im_ref, h_re_ref, h_im_ref, end_ref, *, reverse
):
    rounds, width = a_re_ref.shape
    shots = d_re_ref.shape[0]

    def step(i, carry):
        p_re, p_im, states = carry
        t = rounds - 1 - i if reverse else i
        row = pl.ds(t, 1)
        a_re = a_re_ref[row, :]
        a_im = a_im_ref[row, :]
        next_p_re = p_re * a_re - p_im * a_im
        next_p_im = p_re * a_im + p_im * a_re
        p_re_ref[row, :] = next_p_re
        p_im_ref[row, :] = next_p_im
        moved = []
        for b in range(shots):
            h_re, h_im = states[b]
            new_re = a_re * h_re - a_im * h_im + d_re_ref[b, row, :]
            new_im = a_im * h_re + a_re * h_im + d_im_ref[b, row, :]
            h_re_ref[b, row, :] = new_re
            h_im_ref[b, row, :] = new_im
            moved.append((new_re, new_im))
        return (next_p_re, next_p_im, tuple(moved))

    zero = jnp.zeros((1, width), jnp.float32)
    start = (jnp.ones((1, width), jnp.float32), zero, tuple((zero, zero) for _ in range(shots)))
    p_re, p_im, states = lax.fori_loop(0, rounds, step, start, unroll=8)
    for copy in range(end_ref.shape[0]):
        for b in range(shots):
            end_ref[copy, 0, pl.ds(b, 1), :] = p_re
            end_ref[copy, 1, pl.ds(b, 1), :] = p_im
            end_ref[copy, 2, pl.ds(b, 1), :] = states[b][0]
            end_ref[copy, 3, pl.ds(b, 1), :] = states[b][1]


def recurrence(a_re, a_im, d_re, d_im, reverse=False, copies=1):
    rounds, width = a_re.shape
    shots = d_re.shape[0]
    vmem = pl.BlockSpec(memory_space=pltpu.VMEM)
    coeff = jax.ShapeDtypeStruct((rounds, width), jnp.float32)
    state = jax.ShapeDtypeStruct((shots, rounds, width), jnp.float32)
    return pl.pallas_call(
        functools.partial(_recurrence_kernel, reverse=reverse),
        out_shape=(coeff, coeff, state, state, jax.ShapeDtypeStruct((copies, 4, shots, width), jnp.float32)),
        in_specs=[vmem] * 4,
        out_specs=(vmem,) * 5,
        cost_estimate=pl.CostEstimate(
            flops=8 * rounds * width * (shots + 1),
            transcendentals=0,
            bytes_accessed=4 * 4 * rounds * width * (shots + 1),
        ),
    )(a_re, a_im, d_re, d_im)


def entering(shard, axis, combine, identity, reverse):
    peers, position = (lax.axis_size(axis), lax.axis_index(axis))
    copies = shard
    shard = tuple(copies[0, i] for i in range(copies.shape[1]))
    common = jnp.broadcast_shapes(*(part.shape for part in shard))
    everything = lax.all_to_all(copies, axis, 0, 0, tiled=True)
    state = tuple(
        jnp.broadcast_to(jnp.asarray(zero, part.dtype), common) for part, zero in zip(shard, identity)
    )
    for k in range(peers):
        at = peers - 1 - k if reverse else k
        reached = at > position if reverse else at < position
        new = combine(state, tuple(everything[at, i] for i in range(len(shard))))
        state = tuple(jnp.where(reached, a, b) for a, b in zip(new, state))
    return state


def ring_stage(first, second, axis, n, stride, dim):
    index = lax.axis_index(axis)
    size = lax.axis_size(axis)
    pos = (index // stride) % n

    def moved(j, step):
        at = (j // stride) % n
        return j - at * stride + ((at + step) % n) * stride

    ahead = [(j, moved(j, 1)) for j in range(size)]
    behind = [(j, moved(j, -1)) for j in range(size)]
    chunk = first.shape[dim] // n

    def take(part, c):
        return lax.dynamic_slice_in_dim(part, c * chunk, chunk, dim)

    acc_first = take(first, (pos - 1) % n)
    acc_second = take(second, (pos + 1) % n)
    for step in range(n - 1):
        acc_first = lax.ppermute(acc_first, axis, ahead) + take(first, (pos - step - 2) % n)
        acc_second = lax.ppermute(acc_second, axis, behind) + take(second, (pos + step + 2) % n)
    return jnp.concatenate([acc_first, acc_second], 0)


def reduce_scatter_rows(first, second):
    peers = lax.axis_size("round")
    x = ring_stage(first, second, "dp", lax.axis_size("dp"), 1, 1)
    split = x.reshape(x.shape[0], peers, x.shape[1] // peers, x.shape[2])
    return lax.all_to_all(split, "round", 1, 1, tiled=True).sum(axis=1)


def passed_along(value, axis, steps):
    count = lax.axis_size(axis)
    leading, last = (max(0, -steps), min(count, count - steps))
    return lax.ppermute(value, axis, [(source, source + steps) for source in range(leading, last)])


def combine_pairs(preceding, following):
    first_real, first_imag, first_state_real, first_state_imag = preceding
    second_real, second_imag, second_state_real, second_state_imag = following
    return (
        first_real * second_real - first_imag * second_imag,
        first_real * second_imag + first_imag * second_real,
        second_real * first_state_real - second_imag * first_state_imag + second_state_real,
        second_imag * first_state_real + second_real * first_state_imag + second_state_imag,
    )


def incoming_state(summary, neutral):
    return entering(summary, "round", combine_pairs, neutral, False)


def incoming_adjoint(summary, neutral):
    return entering(summary, "round", combine_pairs, neutral, True)


def neutral_of(summary):
    return (
        jnp.ones_like(summary[0]),
        jnp.zeros_like(summary[1]),
        jnp.zeros_like(summary[2]),
        jnp.zeros_like(summary[3]),
    )


def inverse_rms(values):
    return lax.rsqrt(jnp.mean(values * values, axis=-1, keepdims=True) + 1e-06)


def forward_block(inputs, weight_in, weight_out, trans_real, trans_imag, input_gain, valid_rounds):
    feature_count = inputs.shape[-1]
    widened = inputs.astype(jnp.float32)
    normed = (widened * inverse_rms(widened)).astype(jnp.bfloat16)
    driven = jnp.einsum("brw,wk->brk", normed, weight_in, preferred_element_type=jnp.float32)
    driven = driven * valid_rounds[:, :, None]
    drive_real = driven[:, :, :feature_count] * input_gain
    drive_imag = driven[:, :, feature_count:] * input_gain
    prod_real, prod_imag, local_real, local_imag, ends = recurrence(
        trans_real, trans_imag, drive_real, drive_imag, copies=lax.axis_size("round")
    )
    prod_real, prod_imag = (prod_real[None], prod_imag[None])
    carried = incoming_state(ends, neutral_of(tuple(ends[0, i] for i in range(4))))
    carry_real = carried[2][:, None]
    carry_imag = carried[3][:, None]
    state_real = local_real + prod_real * carry_real - prod_imag * carry_imag
    state_imag = local_imag + prod_real * carry_imag + prod_imag * carry_real
    hidden = jnp.concatenate([state_real, state_imag], axis=-1).astype(jnp.bfloat16)
    mixed = jnp.einsum("brk,kw->brw", hidden, weight_out, preferred_element_type=jnp.float32)
    outputs = (widened + mixed).astype(jnp.bfloat16)
    return (outputs, normed, hidden)


def backward_block(
    inputs,
    normed,
    hidden,
    upstream,
    weight_in,
    weight_out,
    trans_real,
    trans_imag,
    input_gain,
    valid_rounds,
):
    feature_count = inputs.shape[-1]
    upstream_low = upstream.astype(jnp.bfloat16)
    grad_out = jnp.einsum("brk,brw->kw", hidden, upstream_low, preferred_element_type=jnp.float32)
    state_grad = jnp.einsum(
        "brw,kw->brk", upstream_low, weight_out, preferred_element_type=jnp.float32
    )
    error_real = state_grad[:, :, :feature_count]
    error_imag = state_grad[:, :, feature_count:]
    back_real = trans_real[None]
    back_imag = -trans_imag[None]
    pushed_real = back_real * error_real - back_imag * error_imag
    pushed_imag = back_real * error_imag + back_imag * error_real
    suffix_real, suffix_imag, local_real, local_imag, ends = recurrence(
        back_real[0], back_imag[0], pushed_real, pushed_imag, reverse=True, copies=lax.axis_size("round")
    )
    suffix_real, suffix_imag = (suffix_real[None], suffix_imag[None])
    carried = incoming_adjoint(ends, neutral_of(tuple(ends[0, i] for i in range(4))))
    carry_real = carried[2][:, None]
    carry_imag = carried[3][:, None]
    passed_real = local_real + suffix_real * carry_real - suffix_imag * carry_imag
    passed_imag = local_imag + suffix_real * carry_imag + suffix_imag * carry_real
    next_real = jnp.concatenate([passed_real[:, 1:], carry_real], axis=1)
    next_imag = jnp.concatenate([passed_imag[:, 1:], carry_imag], axis=1)
    adjoint_real = error_real + next_real
    adjoint_imag = error_imag + next_imag
    drive_grad = (
        jnp.concatenate([adjoint_real * input_gain, adjoint_imag * input_gain], axis=-1)
        * valid_rounds[:, :, None]
    ).astype(jnp.bfloat16)
    grad_in = jnp.einsum("brk,brw->kw", drive_grad, normed, preferred_element_type=jnp.float32)
    normed_grad = jnp.einsum(
        "brk,wk->brw", drive_grad, weight_in, preferred_element_type=jnp.float32
    )
    widened = inputs.astype(jnp.float32)
    inv_scale = inverse_rms(widened)
    input_grad = upstream + inv_scale * (
        normed_grad
        - widened * inv_scale * inv_scale * jnp.mean(normed_grad * widened, axis=-1, keepdims=True)
    )
    return (grad_in, grad_out, input_grad)


def body(syndromes, lengths, flips, embed, w_in, w_out, leak, angle, readout):
    shots_here = syndromes.shape[0]
    rounds_here = syndromes.shape[2]
    feature_count = embed.shape[1]
    micro_shots = shots_here // MICRO
    shot_total = shots_here * lax.axis_size("dp")
    section_index = lax.axis_index("section")
    first_section = section_index == 0
    positions = lax.axis_index("round") * rounds_here + jnp.arange(rounds_here, dtype=jnp.int32)
    valid_all = (positions[None, :] < lengths[:, None]).astype(jnp.float32)
    weight_in = w_in[0]
    weight_out = w_out[0]
    forget = leak[0]
    decay_factor = jnp.exp(-forget)
    trans_real = decay_factor * jnp.cos(angle[0])[None, :]
    trans_imag = decay_factor * jnp.sin(angle[0])[None, :]
    input_gain = jnp.sqrt(-jnp.expm1(-2.0 * forget))
    readout_wide = readout.astype(jnp.float32)
    received = jnp.zeros((micro_shots, rounds_here, feature_count), jnp.bfloat16)
    saved_ticks = []
    loss_grads = []
    for tick_index in range(MICRO + 1):
        own_index = min(tick_index, MICRO - 1)
        syndrome_bits = syndromes[own_index * micro_shots : (own_index + 1) * micro_shots].astype(
            jnp.bfloat16
        )
        embedded = jnp.einsum(
            "bsr,sw->brw", syndrome_bits, embed, preferred_element_type=jnp.float32
        ).astype(jnp.bfloat16)
        inputs = jnp.where(first_section, embedded, received)
        micro_index = jnp.clip(tick_index - section_index, 0, MICRO - 1)
        valid_rounds = lax.dynamic_slice_in_dim(
            valid_all, micro_index * micro_shots, micro_shots, 0
        )
        outputs, normed, hidden = forward_block(
            inputs, weight_in, weight_out, trans_real, trans_imag, input_gain, valid_rounds
        )
        saved_ticks.append((inputs, normed, hidden, valid_rounds))
        if tick_index >= 1:
            logits = jnp.einsum("brw,w->br", outputs, readout, preferred_element_type=jnp.float32)
            targets = flips[(tick_index - 1) * micro_shots : tick_index * micro_shots].astype(
                jnp.float32
            )
            scaled = (jax.nn.sigmoid(logits) - targets) * valid_rounds / shot_total
            loss_grads.append(scaled[:, :, None] * readout_wide)
        if tick_index < MICRO:
            received = passed_along(outputs, "section", 1)
    grad_in_sum = jnp.zeros((2 * feature_count, feature_count), jnp.float32)
    grad_out_sum = jnp.zeros((2 * feature_count, feature_count), jnp.float32)
    arriving = jnp.zeros((micro_shots, rounds_here, feature_count), jnp.bfloat16)
    for tick_index in range(MICRO + 1):
        later_saved = saved_ticks[min(tick_index + 1, MICRO)]
        earlier = saved_ticks[max(tick_index - 1, 0)]
        picked = tuple(
            (jnp.where(first_section, lower, higher) for higher, lower in zip(later_saved, earlier))
        )
        own_grad = (
            loss_grads[tick_index]
            if tick_index < MICRO
            else jnp.zeros((micro_shots, rounds_here, feature_count), jnp.float32)
        )
        upstream = jnp.where(first_section, arriving.astype(jnp.float32), own_grad)
        grad_in_part, grad_out_part, input_grad = backward_block(
            picked[0],
            picked[1],
            picked[2],
            upstream,
            weight_in,
            weight_out,
            trans_real,
            trans_imag,
            input_gain,
            picked[3],
        )
        grad_in_sum = grad_in_sum + grad_in_part
        grad_out_sum = grad_out_sum + grad_out_part
        if tick_index < MICRO:
            arriving = passed_along(input_grad.astype(jnp.bfloat16), "section", -1)
    reduced = reduce_scatter_rows(grad_in_sum[None], grad_out_sum[None])
    return (jnp.swapaxes(reduced[0:1], 1, 2), reduced[1:2])


def solution(mesh):
    return jax.shard_map(
        body,
        mesh=mesh,
        in_specs=(
            P("dp", None, "round"),
            P("dp"),
            P("dp", "round"),
            P(),
            P("section", None, None),
            P("section", None, None),
            P("section", "round", None),
            P("section", None),
            P(),
        ),
        out_specs=(P("section", None, ("dp", "round")), P("section", ("dp", "round"), None)),
        check_vma=False,
    )
```

```python
import functools

import jax
import jax.numpy as jnp
from jax import lax
from jax.experimental import pallas as pl
from jax.experimental.pallas import tpu as pltpu
from jax.sharding import PartitionSpec as P

MICRO = 1


def _recurrence_kernel(
    a_re_ref, a_im_ref, d_re_ref, d_im_ref, p_re_ref, p_im_ref, h_re_ref, h_im_ref, end_ref, *, reverse
):
    rounds, width = a_re_ref.shape
    shots = d_re_ref.shape[0]

    def step(i, carry):
        p_re, p_im, states = carry
        t = rounds - 1 - i if reverse else i
        row = pl.ds(t, 1)
        a_re = a_re_ref[row, :]
        a_im = a_im_ref[row, :]
        next_p_re = p_re * a_re - p_im * a_im
        next_p_im = p_re * a_im + p_im * a_re
        p_re_ref[row, :] = next_p_re
        p_im_ref[row, :] = next_p_im
        moved = []
        for b in range(shots):
            h_re, h_im = states[b]
            new_re = a_re * h_re - a_im * h_im + d_re_ref[b, row, :]
            new_im = a_im * h_re + a_re * h_im + d_im_ref[b, row, :]
            h_re_ref[b, row, :] = new_re
            h_im_ref[b, row, :] = new_im
            moved.append((new_re, new_im))
        return (next_p_re, next_p_im, tuple(moved))

    zero = jnp.zeros((1, width), jnp.float32)
    start = (jnp.ones((1, width), jnp.float32), zero, tuple((zero, zero) for _ in range(shots)))
    p_re, p_im, states = lax.fori_loop(0, rounds, step, start, unroll=16)
    for copy in range(end_ref.shape[0]):
        for b in range(shots):
            end_ref[copy, 0, pl.ds(b, 1), :] = p_re
            end_ref[copy, 1, pl.ds(b, 1), :] = p_im
            end_ref[copy, 2, pl.ds(b, 1), :] = states[b][0]
            end_ref[copy, 3, pl.ds(b, 1), :] = states[b][1]


def recurrence(a_re, a_im, d_re, d_im, reverse=False, copies=1):
    rounds, width = a_re.shape
    shots = d_re.shape[0]
    vmem = pl.BlockSpec(memory_space=pltpu.VMEM)
    coeff = jax.ShapeDtypeStruct((rounds, width), jnp.float32)
    state = jax.ShapeDtypeStruct((shots, rounds, width), jnp.float32)
    return pl.pallas_call(
        functools.partial(_recurrence_kernel, reverse=reverse),
        out_shape=(coeff, coeff, state, state, jax.ShapeDtypeStruct((copies, 4, shots, width), jnp.float32)),
        in_specs=[vmem] * 4,
        out_specs=(vmem,) * 5,
        cost_estimate=pl.CostEstimate(
            flops=8 * rounds * width * (shots + 1),
            transcendentals=0,
            bytes_accessed=4 * 4 * rounds * width * (shots + 1),
        ),
    )(a_re, a_im, d_re, d_im)


def entering(shard, axis, combine, identity, reverse):
    peers, position = (lax.axis_size(axis), lax.axis_index(axis))
    copies = shard
    shard = tuple(copies[0, i] for i in range(copies.shape[1]))
    common = jnp.broadcast_shapes(*(part.shape for part in shard))
    everything = lax.all_to_all(copies, axis, 0, 0, tiled=True)
    state = tuple(
        jnp.broadcast_to(jnp.asarray(zero, part.dtype), common) for part, zero in zip(shard, identity)
    )
    for k in range(peers):
        at = peers - 1 - k if reverse else k
        reached = at > position if reverse else at < position
        new = combine(state, tuple(everything[at, i] for i in range(len(shard))))
        state = tuple(jnp.where(reached, a, b) for a, b in zip(new, state))
    return state


def ring_stage(first, second, axis, n, stride, dim):
    index = lax.axis_index(axis)
    size = lax.axis_size(axis)
    pos = (index // stride) % n

    def moved(j, step):
        at = (j // stride) % n
        return j - at * stride + ((at + step) % n) * stride

    ahead = [(j, moved(j, 1)) for j in range(size)]
    behind = [(j, moved(j, -1)) for j in range(size)]
    chunk = first.shape[dim] // n

    def take(part, c):
        return lax.dynamic_slice_in_dim(part, c * chunk, chunk, dim)

    acc_first = take(first, (pos - 1) % n)
    acc_second = take(second, (pos + 1) % n)
    for step in range(n - 1):
        acc_first = lax.ppermute(acc_first, axis, ahead) + take(first, (pos - step - 2) % n)
        acc_second = lax.ppermute(acc_second, axis, behind) + take(second, (pos + step + 2) % n)
    return jnp.concatenate([acc_first, acc_second], 0)


def reduce_scatter_rows(first, second):
    peers = lax.axis_size("round")
    x = ring_stage(first, second, "dp", lax.axis_size("dp"), 1, 1)
    split = x.reshape(x.shape[0], peers, x.shape[1] // peers, x.shape[2])
    return lax.all_to_all(split, "round", 1, 1, tiled=True).sum(axis=1)


def passed_along(value, axis, steps):
    count = lax.axis_size(axis)
    leading, last = (max(0, -steps), min(count, count - steps))
    return lax.ppermute(value, axis, [(source, source + steps) for source in range(leading, last)])


def combine_pairs(preceding, following):
    first_real, first_imag, first_state_real, first_state_imag = preceding
    second_real, second_imag, second_state_real, second_state_imag = following
    return (
        first_real * second_real - first_imag * second_imag,
        first_real * second_imag + first_imag * second_real,
        second_real * first_state_real - second_imag * first_state_imag + second_state_real,
        second_imag * first_state_real + second_real * first_state_imag + second_state_imag,
    )


def incoming_state(summary, neutral):
    return entering(summary, "round", combine_pairs, neutral, False)


def incoming_adjoint(summary, neutral):
    return entering(summary, "round", combine_pairs, neutral, True)


def neutral_of(summary):
    return (
        jnp.ones_like(summary[0]),
        jnp.zeros_like(summary[1]),
        jnp.zeros_like(summary[2]),
        jnp.zeros_like(summary[3]),
    )


def inverse_rms(values):
    return lax.rsqrt(jnp.mean(values * values, axis=-1, keepdims=True) + 1e-06)


def forward_block(inputs, weight_in, weight_out, trans_real, trans_imag, input_gain, valid_rounds):
    feature_count = inputs.shape[-1]
    widened = inputs.astype(jnp.float32)
    normed = (widened * inverse_rms(widened)).astype(jnp.bfloat16)
    driven = jnp.einsum("brw,wk->brk", normed, weight_in, preferred_element_type=jnp.float32)
    driven = driven * valid_rounds[:, :, None]
    drive_real = driven[:, :, :feature_count] * input_gain
    drive_imag = driven[:, :, feature_count:] * input_gain
    prod_real, prod_imag, local_real, local_imag, ends = recurrence(
        trans_real, trans_imag, drive_real, drive_imag, copies=lax.axis_size("round")
    )
    prod_real, prod_imag = (prod_real[None], prod_imag[None])
    carried = incoming_state(ends, neutral_of(tuple(ends[0, i] for i in range(4))))
    carry_real = carried[2][:, None]
    carry_imag = carried[3][:, None]
    state_real = local_real + prod_real * carry_real - prod_imag * carry_imag
    state_imag = local_imag + prod_real * carry_imag + prod_imag * carry_real
    hidden = jnp.concatenate([state_real, state_imag], axis=-1).astype(jnp.bfloat16)
    mixed = jnp.einsum("brk,kw->brw", hidden, weight_out, preferred_element_type=jnp.float32)
    outputs = (widened + mixed).astype(jnp.bfloat16)
    return (outputs, normed, hidden)


def backward_block(
    inputs,
    normed,
    hidden,
    upstream,
    weight_in,
    weight_out,
    trans_real,
    trans_imag,
    input_gain,
    valid_rounds,
):
    feature_count = inputs.shape[-1]
    upstream_low = upstream.astype(jnp.bfloat16)
    grad_out = jnp.einsum("brk,brw->kw", hidden, upstream_low, preferred_element_type=jnp.float32)
    state_grad = jnp.einsum(
        "brw,kw->brk", upstream_low, weight_out, preferred_element_type=jnp.float32
    )
    error_real = state_grad[:, :, :feature_count]
    error_imag = state_grad[:, :, feature_count:]
    back_real = trans_real[None]
    back_imag = -trans_imag[None]
    pushed_real = back_real * error_real - back_imag * error_imag
    pushed_imag = back_real * error_imag + back_imag * error_real
    suffix_real, suffix_imag, local_real, local_imag, ends = recurrence(
        back_real[0], back_imag[0], pushed_real, pushed_imag, reverse=True, copies=lax.axis_size("round")
    )
    suffix_real, suffix_imag = (suffix_real[None], suffix_imag[None])
    carried = incoming_adjoint(ends, neutral_of(tuple(ends[0, i] for i in range(4))))
    carry_real = carried[2][:, None]
    carry_imag = carried[3][:, None]
    passed_real = local_real + suffix_real * carry_real - suffix_imag * carry_imag
    passed_imag = local_imag + suffix_real * carry_imag + suffix_imag * carry_real
    next_real = jnp.concatenate([passed_real[:, 1:], carry_real], axis=1)
    next_imag = jnp.concatenate([passed_imag[:, 1:], carry_imag], axis=1)
    adjoint_real = error_real + next_real
    adjoint_imag = error_imag + next_imag
    drive_grad = (
        jnp.concatenate([adjoint_real * input_gain, adjoint_imag * input_gain], axis=-1)
        * valid_rounds[:, :, None]
    ).astype(jnp.bfloat16)
    grad_in = jnp.einsum("brk,brw->kw", drive_grad, normed, preferred_element_type=jnp.float32)
    normed_grad = jnp.einsum(
        "brk,wk->brw", drive_grad, weight_in, preferred_element_type=jnp.float32
    )
    widened = inputs.astype(jnp.float32)
    inv_scale = inverse_rms(widened)
    input_grad = upstream + inv_scale * (
        normed_grad
        - widened * inv_scale * inv_scale * jnp.mean(normed_grad * widened, axis=-1, keepdims=True)
    )
    return (grad_in, grad_out, input_grad)


def body(syndromes, lengths, flips, embed, w_in, w_out, leak, angle, readout):
    shots_here = syndromes.shape[0]
    rounds_here = syndromes.shape[2]
    feature_count = embed.shape[1]
    micro_shots = shots_here // MICRO
    shot_total = shots_here * lax.axis_size("dp")
    section_index = lax.axis_index("section")
    first_section = section_index == 0
    positions = lax.axis_index("round") * rounds_here + jnp.arange(rounds_here, dtype=jnp.int32)
    valid_all = (positions[None, :] < lengths[:, None]).astype(jnp.float32)
    weight_in = w_in[0]
    weight_out = w_out[0]
    forget = leak[0]
    decay_factor = jnp.exp(-forget)
    trans_real = decay_factor * jnp.cos(angle[0])[None, :]
    trans_imag = decay_factor * jnp.sin(angle[0])[None, :]
    input_gain = jnp.sqrt(-jnp.expm1(-2.0 * forget))
    readout_wide = readout.astype(jnp.float32)
    received = jnp.zeros((micro_shots, rounds_here, feature_count), jnp.bfloat16)
    saved_ticks = []
    loss_grads = []
    for tick_index in range(MICRO + 1):
        own_index = min(tick_index, MICRO - 1)
        syndrome_bits = syndromes[own_index * micro_shots : (own_index + 1) * micro_shots].astype(
            jnp.bfloat16
        )
        embedded = jnp.einsum(
            "bsr,sw->brw", syndrome_bits, embed, preferred_element_type=jnp.float32
        ).astype(jnp.bfloat16)
        inputs = jnp.where(first_section, embedded, received)
        micro_index = jnp.clip(tick_index - section_index, 0, MICRO - 1)
        valid_rounds = lax.dynamic_slice_in_dim(
            valid_all, micro_index * micro_shots, micro_shots, 0
        )
        outputs, normed, hidden = forward_block(
            inputs, weight_in, weight_out, trans_real, trans_imag, input_gain, valid_rounds
        )
        saved_ticks.append((inputs, normed, hidden, valid_rounds))
        if tick_index >= 1:
            logits = jnp.einsum("brw,w->br", outputs, readout, preferred_element_type=jnp.float32)
            targets = flips[(tick_index - 1) * micro_shots : tick_index * micro_shots].astype(
                jnp.float32
            )
            scaled = (jax.nn.sigmoid(logits) - targets) * valid_rounds / shot_total
            loss_grads.append(scaled[:, :, None] * readout_wide)
        if tick_index < MICRO:
            received = passed_along(outputs, "section", 1)
    grad_in_sum = jnp.zeros((2 * feature_count, feature_count), jnp.float32)
    grad_out_sum = jnp.zeros((2 * feature_count, feature_count), jnp.float32)
    arriving = jnp.zeros((micro_shots, rounds_here, feature_count), jnp.bfloat16)
    for tick_index in range(MICRO + 1):
        later_saved = saved_ticks[min(tick_index + 1, MICRO)]
        earlier = saved_ticks[max(tick_index - 1, 0)]
        picked = tuple(
            (jnp.where(first_section, lower, higher) for higher, lower in zip(later_saved, earlier))
        )
        own_grad = (
            loss_grads[tick_index]
            if tick_index < MICRO
            else jnp.zeros((micro_shots, rounds_here, feature_count), jnp.float32)
        )
        upstream = jnp.where(first_section, arriving.astype(jnp.float32), own_grad)
        grad_in_part, grad_out_part, input_grad = backward_block(
            picked[0],
            picked[1],
            picked[2],
            upstream,
            weight_in,
            weight_out,
            trans_real,
            trans_imag,
            input_gain,
            picked[3],
        )
        grad_in_sum = grad_in_sum + grad_in_part
        grad_out_sum = grad_out_sum + grad_out_part
        if tick_index < MICRO:
            arriving = passed_along(input_grad.astype(jnp.bfloat16), "section", -1)
    reduced = reduce_scatter_rows(grad_in_sum[None], grad_out_sum[None])
    return (jnp.swapaxes(reduced[0:1], 1, 2), reduced[1:2])


def solution(mesh):
    return jax.shard_map(
        body,
        mesh=mesh,
        in_specs=(
            P("dp", None, "round"),
            P("dp"),
            P("dp", "round"),
            P(),
            P("section", None, None),
            P("section", None, None),
            P("section", "round", None),
            P("section", None),
            P(),
        ),
        out_specs=(P("section", None, ("dp", "round")), P("section", ("dp", "round"), None)),
        check_vma=False,
    )
```
